32 devices in a mesh: groups: 2 (over x), tok: 16 (over z, y, core).
Axes of the slice: x: 2, y: 2, z: 4, core: 2. Of those that a mesh axis runs over, the one named last changes fastest.
Arguments:
- queries: bfloat16 [2, 8192, 1024], P(None, ('groups', 'tok')), parts along dimension 1, may hold values from -6 to 6
- keys: bfloat16 [2, 8192, 1024], P(None, ('groups', 'tok')), parts along dimension 1, may hold values from -6 to 6
- values: bfloat16 [2, 8192, 1024], P(None, ('groups', 'tok')), parts along dimension 1, may hold values from -6 to 6
- rates: float32 [2, 3, 2, 8192], P(None, None, None, ('groups', 'tok')), parts along dimension 3, may hold values from 0.0002 to 0.002
- fast_weights: float32 [2, 3, 512, 512], P(None, None, 'tok'), may hold values from -0.25 to 0.25
Outputs:
- attended: bfloat16 [2, 8192, 1024], P(None, ('groups', 'tok')), parts along dimension 1
- final_weights: float32 [4, 3, 512, 512], P('groups', None, 'tok'), parts along dimension 0
The draws below stay inside these ranges and needn't reach their ends.
There are 2 independent parts, one for each index of `groups`. The reference program is written for one: setup_inputs(seed, part) draws one part's arguments, and reference() takes and returns one part's arrays. A program takes and returns all parts, laid end to end along the dimension named above; an argument that names none is the same for every part. Nothing has to cross between parts.
All inputs are finite; a program needn't handle non-finite values.
Results may differ from the reference program's by a relative error of at most 0.0098.
Values may be sent and summed in bfloat16 or wider, within the bound.
No kernel may reach another device: no remote copies, remote signals or barrier semaphores. Data moves between devices by JAX's collectives and lax.ppermute only.
A program may use at most 64 MiB of HBM per device.

```python
import math
import jax
import jax.numpy as jnp
from jax import lax

H = 2
DH = 512
HID = 512
NCHUNK = 2
SPAN = 4096
WIDTH = 1024


def level_of(key, extent, cuts, least, largest):
    loudness = 1.0
    for position, parts in cuts:
        draws = jax.random.uniform(jax.random.fold_in(jax.random.fold_in(key, 6), position), (parts,), jnp.float32, least / len(cuts), largest / len(cuts))
        loudness = loudness * jnp.repeat(jnp.exp(draws), extent[position] // parts).reshape((-1,) + (1,) * (len(extent) - 1 - position))
    return loudness


def bell_draw(own_key, shape, spread, bound, shards=(), held_as=jnp.bfloat16):
    array = jax.random.normal(own_key, shape, jnp.float32) * spread
    if len(shards) > 0:
        array = level_of(own_key, shape, shards, -0.22, 0.18) * array
    return jnp.clip(array, min=-bound, max=bound).astype(held_as)


def setup_inputs(seed: int = 0, part: int = 0) -> dict:
    key_list = jax.random.split(jax.random.key(seed), 6)
    own_keys = jax.random.split(jax.random.fold_in(key_list[5], part), 6)
    queries = bell_draw(own_keys[0], (NCHUNK, SPAN, WIDTH), 1.0, 6.0, ((1, 16),))
    keys = bell_draw(own_keys[1], (NCHUNK, SPAN, WIDTH), 1.0, 6.0, ((1, 16),))
    values = bell_draw(own_keys[2], (NCHUNK, SPAN, WIDTH), 1.0, 6.0, ((1, 16),))
    rates = jnp.clip(jnp.exp(math.log(0.002) - 2.3025852 * jax.random.uniform(own_keys[3], (NCHUNK, 3, H, SPAN), jnp.float32) ** level_of(own_keys[3], (NCHUNK, 3, H, SPAN), ((3, 16),), -0.2, 0.2)), 0.0002, 0.002)
    fast_weights = bell_draw(key_list[4], (H, 3, HID, DH), DH ** -0.5, 0.25, ((2, 16),), jnp.float32)
    return dict(queries=queries, keys=keys, values=values, rates=rates, fast_weights=fast_weights)


def cross(left, right):
    return lax.dot_general(left, right, (((1,), (1,)), ((), ())), preferred_element_type=jnp.float32)

def inner(left, right):
    return lax.dot_general(left, right, (((0,), (0,)), ((), ())), preferred_element_type=jnp.float32)

def renorm(old, upd):
    old_norm = jnp.sqrt(lax.optimization_barrier(jnp.mean(old * old, axis=-1)))
    new_norm = jnp.sqrt(lax.optimization_barrier(jnp.mean(upd * upd, axis=-1)) + 1e-06)
    return upd * (old_norm / new_norm)[..., None]

def head_step(query, key_rows, value_rows, rate_rows, wbf):
    hidden_q = (jax.nn.silu(cross(query, wbf[0])) * cross(query, wbf[1])).astype(jnp.bfloat16)
    raw = cross(hidden_q, wbf[2])
    normed = (raw / jnp.sqrt(lax.optimization_barrier(jnp.mean(raw * raw, axis=-1, keepdims=True)) + 1e-06)).astype(jnp.bfloat16)
    h1 = cross(key_rows, wbf[0])
    h3 = cross(key_rows, wbf[1])
    sig = jax.nn.sigmoid(h1)
    act = h1 * sig
    back = jnp.dot(value_rows, wbf[2], preferred_element_type=jnp.float32)
    d1 = back * h3 * sig * (1.0 + h1 * (1.0 - sig))
    d3 = back * act
    e1 = (rate_rows[0][:, None] * d1).astype(jnp.bfloat16)
    e3 = (rate_rows[1][:, None] * d3).astype(jnp.bfloat16)
    b2 = (rate_rows[2][:, None] * (act * h3)).astype(jnp.bfloat16)
    grad = jnp.stack([inner(e1, key_rows), inner(e3, key_rows), inner(value_rows, b2)])
    return (normed, grad)

def reference(queries, keys, values, rates, fast_weights):
    weights = fast_weights
    blocks = []
    for span in range(NCHUNK):
        wbf = weights.astype(jnp.bfloat16)
        pieces = []
        grads = []
        for head in range(H):
            lo = head * DH
            normed, grad = head_step(queries[span][:, lo:lo + DH], keys[span][:, lo:lo + DH], values[span][:, lo:lo + DH], rates[span][:, head], wbf[head])
            pieces.append(normed)
            grads.append(grad)
        blocks.append(jnp.concatenate(pieces, axis=1))
        weights = renorm(weights, weights + jnp.stack(grads))
    return (jnp.stack(blocks), weights)
```

```python
import jax
import jax.numpy as jnp
from jax import lax
from jax.sharding import PartitionSpec as P


def cross(left, right):
    return lax.dot_general(
        left, right, (((1,), (1,)), ((), ())), preferred_element_type=jnp.float32
    )


def inner(left, right):
    return lax.dot_general(
        left, right, (((0,), (0,)), ((), ())), preferred_element_type=jnp.float32
    )


def renorm(old, upd):
    old_norm = jnp.sqrt(jnp.mean(old * old, axis=-1))
    new_norm = jnp.sqrt(jnp.mean(upd * upd, axis=-1) + 1e-06)
    return upd * (old_norm / new_norm)[..., None]


def head_step(query, key_rows, value_rows, rate_rows, wbf):
    hidden_q = (jax.nn.silu(cross(query, wbf[0])) * cross(query, wbf[1])).astype(jnp.bfloat16)
    raw = cross(hidden_q, wbf[2])
    normed = (raw / jnp.sqrt(jnp.mean(raw * raw, axis=-1, keepdims=True) + 1e-06)).astype(
        jnp.bfloat16
    )
    h1 = cross(key_rows, wbf[0])
    h3 = cross(key_rows, wbf[1])
    sig = jax.nn.sigmoid(h1)
    act = h1 * sig
    back = jnp.dot(value_rows, wbf[2], preferred_element_type=jnp.float32)
    d1 = back * h3 * sig * (1.0 + h1 * (1.0 - sig))
    d3 = back * act
    e1 = (rate_rows[0][:, None] * d1).astype(jnp.bfloat16)
    e3 = (rate_rows[1][:, None] * d3).astype(jnp.bfloat16)
    b2 = (rate_rows[2][:, None] * (act * h3)).astype(jnp.bfloat16)
    grad = jnp.stack([inner(e1, key_rows), inner(e3, key_rows), inner(value_rows, b2)])
    return (normed, grad)


def block_step(span, gathered, queries, keys, values, rates):
    heads = gathered.shape[0]
    width = gathered.shape[3]
    pieces = []
    grads = []
    for head in range(heads):
        lo = head * width
        normed, grad = head_step(
            queries[span][:, lo : lo + width],
            keys[span][:, lo : lo + width],
            values[span][:, lo : lo + width],
            rates[span][:, head],
            gathered[head],
        )
        pieces.append(normed)
        grads.append(grad)
    return (jnp.concatenate(pieces, axis=1), jnp.stack(grads))


class Ring:
    def __init__(self, mesh):
        tok = mesh.shape["tok"]
        chips = tok // 2
        coords = [tuple(mesh.devices[0, 2 * c].coords) for c in range(chips)]
        ys = sorted({c[1] for c in coords})
        if len(ys) == 2:
            ahead = sorted((c for c in range(chips) if coords[c][1] == ys[0]), key=lambda c: coords[c][2])
            back = sorted((c for c in range(chips) if coords[c][1] == ys[1]), key=lambda c: -coords[c][2])
            cycle = ahead + back
        else:
            cycle = sorted(range(chips), key=lambda c: (coords[c][1], coords[c][2]))
        self.chips = chips
        self.cycle = cycle
        place = [0] * chips
        for i, c in enumerate(cycle):
            place[c] = i
        self.place = place
        self.cw = [(cycle[p] * 2 + k, cycle[(p + 1) % chips] * 2 + k) for p in range(chips) for k in range(2)]
        self.ccw = [(cycle[p] * 2 + k, cycle[(p - 1) % chips] * 2 + k) for p in range(chips) for k in range(2)]
        self.swap = [(t, t ^ 1) for t in range(tok)]
        self.ncw = chips // 2
        self.nccw = chips - 1 - self.ncw

    def chip_at(self, step):
        me = lax.axis_index("tok") // 2
        where = jnp.array(self.place, jnp.int32)[me]
        return jnp.array(self.cycle, jnp.int32)[(where + step) % self.chips]

    def gather(self, own):
        h, g, rows, f = own.shape
        core = lax.axis_index("tok") % 2
        full = jnp.zeros((self.chips, 2, h, g, rows, f), own.dtype)

        def put(full, piece, chip):
            full = lax.dynamic_update_slice(full, piece[None, None], (chip, core, 0, 0, 0, 0))
            other = lax.ppermute(piece, "tok", self.swap)
            return lax.dynamic_update_slice(full, other[None, None], (chip, 1 - core, 0, 0, 0, 0))

        full = put(full, own, lax.axis_index("tok") // 2)
        a = own
        b = own
        for k in range(1, max(self.ncw, self.nccw) + 1):
            if k <= self.ncw:
                a = lax.ppermute(a, "tok", self.cw)
                full = put(full, a, self.chip_at(-k))
            if k <= self.nccw:
                b = lax.ppermute(b, "tok", self.ccw)
                full = put(full, b, self.chip_at(k))
        full = jnp.moveaxis(full, (0, 1), (2, 3))
        return full.reshape(h, g, self.chips * 2 * rows, f)

    def reduce(self, part):
        h, g, r, f = part.shape
        rows = r // (2 * self.chips)
        q = part.reshape(h, g, self.chips, 2, rows, f)
        core = lax.axis_index("tok") % 2

        def chip_sum(step):
            chip = self.chip_at(step)
            keep = lax.dynamic_slice(q, (0, 0, chip, core, 0, 0), (h, g, 1, 1, rows, f))
            send = lax.dynamic_slice(q, (0, 0, chip, 1 - core, 0, 0), (h, g, 1, 1, rows, f))
            got = lax.ppermute(send, "tok", self.swap)
            return (keep + got).reshape(h, g, rows, f)

        total = chip_sum(0)
        a = chip_sum(self.ncw) if self.ncw else None
        b = chip_sum(-self.nccw) if self.nccw else None
        for k in range(1, max(self.ncw, self.nccw) + 1):
            if k <= self.ncw:
                a = lax.ppermute(a, "tok", self.cw)
                if k < self.ncw:
                    a = a + chip_sum(self.ncw - k)
            if k <= self.nccw:
                b = lax.ppermute(b, "tok", self.ccw)
                if k < self.nccw:
                    b = b + chip_sum(-self.nccw + k)
        if a is not None:
            total = total + a
        if b is not None:
            total = total + b
        return total


def solution(mesh):
    ring = Ring(mesh)

    def on_device(queries, keys, values, rates, fast_weights):
        nblocks = queries.shape[0]
        own = fast_weights
        blocks = []
        for span in range(nblocks):
            gathered = ring.gather(own.astype(jnp.bfloat16))
            normed, partial_value = block_step(span, gathered, queries, keys, values, rates)
            blocks.append(normed)
            own = renorm(own, own + ring.reduce(partial_value))
        return (jnp.stack(blocks), own)

    placed = (
        P(None, ("groups", "tok"), None),
        P(None, ("groups", "tok"), None),
        P(None, ("groups", "tok"), None),
        P(None, None, None, ("groups", "tok")),
        P(None, None, "tok", None),
    )
    return jax.shard_map(
        on_device,
        mesh=mesh,
        in_specs=placed,
        out_specs=(P(None, ("groups", "tok"), None), P("groups", None, "tok", None)),
        check_vma=False,
    )
```

```python
import jax
import jax.numpy as jnp
from jax import lax
from jax.sharding import PartitionSpec as P


def cross(left, right):
    return lax.dot_general(
        left, right, (((1,), (1,)), ((), ())), preferred_element_type=jnp.float32
    )


def inner(left, right):
    return lax.dot_general(
        left, right, (((0,), (0,)), ((), ())), preferred_element_type=jnp.float32
    )


def renorm(old, upd):
    old_norm = jnp.sqrt(jnp.mean(old * old, axis=-1))
    new_norm = jnp.sqrt(jnp.mean(upd * upd, axis=-1) + 1e-06)
    return upd * (old_norm / new_norm)[..., None]


def head_step(query, key_rows, value_rows, rate_rows, wbf):
    hidden_q = (jax.nn.silu(cross(query, wbf[0])) * cross(query, wbf[1])).astype(jnp.bfloat16)
    raw = cross(hidden_q, wbf[2])
    normed = (raw / jnp.sqrt(jnp.mean(raw * raw, axis=-1, keepdims=True) + 1e-06)).astype(
        jnp.bfloat16
    )
    h1 = cross(key_rows, wbf[0])
    h3 = cross(key_rows, wbf[1])
    sig = jax.nn.sigmoid(h1)
    act = h1 * sig
    back = jnp.dot(value_rows, wbf[2], preferred_element_type=jnp.float32)
    d1 = back * h3 * sig * (1.0 + h1 * (1.0 - sig))
    d3 = back * act
    e1 = (rate_rows[0][:, None] * d1).astype(jnp.bfloat16)
    e3 = (rate_rows[1][:, None] * d3).astype(jnp.bfloat16)
    b2 = (rate_rows[2][:, None] * (act * h3)).astype(jnp.bfloat16)
    grad = jnp.stack([inner(e1, key_rows), inner(e3, key_rows), inner(value_rows, b2)])
    return (normed, grad)


def block_step(span, gathered, queries, keys, values, rates):
    heads = gathered.shape[0]
    width = gathered.shape[3]
    pieces = []
    grads = []
    for head in range(heads):
        lo = head * width
        normed, grad = head_step(
            queries[span][:, lo : lo + width],
            keys[span][:, lo : lo + width],
            values[span][:, lo : lo + width],
            rates[span][:, head],
            gathered[head],
        )
        pieces.append(normed)
        grads.append(grad)
    return (jnp.concatenate(pieces, axis=1), jnp.stack(grads))


class Ring:
    def __init__(self, mesh):
        tok = mesh.shape["tok"]
        chips = tok // 2
        coords = [tuple(mesh.devices[0, 2 * c].coords) for c in range(chips)]
        ys = sorted({c[1] for c in coords})
        if len(ys) == 2:
            ahead = sorted((c for c in range(chips) if coords[c][1] == ys[0]), key=lambda c: coords[c][2])
            back = sorted((c for c in range(chips) if coords[c][1] == ys[1]), key=lambda c: -coords[c][2])
            cycle = ahead + back
        else:
            cycle = sorted(range(chips), key=lambda c: (coords[c][1], coords[c][2]))
        self.chips = chips
        self.cycle = cycle
        place = [0] * chips
        for i, c in enumerate(cycle):
            place[c] = i
        self.place = place
        self.cw = [(cycle[p] * 2 + k, cycle[(p + 1) % chips] * 2 + k) for p in range(chips) for k in range(2)]
        self.ccw = [(cycle[p] * 2 + k, cycle[(p - 1) % chips] * 2 + k) for p in range(chips) for k in range(2)]
        self.swap = [(t, t ^ 1) for t in range(tok)]
        self.ncw = chips // 2
        self.nccw = chips - 1 - self.ncw

    def chip_at(self, step):
        me = lax.axis_index("tok") // 2
        where = jnp.array(self.place, jnp.int32)[me]
        return jnp.array(self.cycle, jnp.int32)[(where + step) % self.chips]

    def gather(self, own):
        h, g, rows, f = own.shape
        core = lax.axis_index("tok") % 2
        full = jnp.zeros((self.chips, 2, h, g, rows, f), own.dtype)

        def put(full, piece, chip):
            full = lax.dynamic_update_slice(full, piece[None, None], (chip, core, 0, 0, 0, 0))
            other = lax.ppermute(piece, "tok", self.swap)
            return lax.dynamic_update_slice(full, other[None, None], (chip, 1 - core, 0, 0, 0, 0))

        full = put(full, own, lax.axis_index("tok") // 2)
        a = own
        b = own
        for k in range(1, max(self.ncw, self.nccw) + 1):
            if k <= self.ncw:
                a = lax.ppermute(a, "tok", self.cw)
                full = put(full, a, self.chip_at(-k))
            if k <= self.nccw:
                b = lax.ppermute(b, "tok", self.ccw)
                full = put(full, b, self.chip_at(k))
        full = jnp.moveaxis(full, (0, 1), (2, 3))
        return full.reshape(h, g, self.chips * 2 * rows, f)

    def reduce(self, part):
        h, g, r, f = part.shape
        rows = r // (2 * self.chips)
        q = part.reshape(h, g, self.chips, 2, rows, f)
        core = lax.axis_index("tok") % 2

        def chip_sum(step):
            chip = self.chip_at(step)
            keep = lax.dynamic_slice(q, (0, 0, chip, core, 0, 0), (h, g, 1, 1, rows, f))
            send = lax.dynamic_slice(q, (0, 0, chip, 1 - core, 0, 0), (h, g, 1, 1, rows, f))
            got = lax.ppermute(send, "tok", self.swap)
            return (keep + got).reshape(h, g, rows, f)

        total = chip_sum(0)
        a = chip_sum(self.ncw) if self.ncw else None
        b = chip_sum(-self.nccw) if self.nccw else None
        for k in range(1, max(self.ncw, self.nccw) + 1):
            if k <= self.ncw:
                a = lax.ppermute(a.astype(jnp.bfloat16), "tok", self.cw).astype(jnp.float32)
                if k < self.ncw:
                    a = a + chip_sum(self.ncw - k)
            if k <= self.nccw:
                b = lax.ppermute(b.astype(jnp.bfloat16), "tok", self.ccw).astype(jnp.float32)
                if k < self.nccw:
                    b = b + chip_sum(-self.nccw + k)
        if a is not None:
            total = total + a
        if b is not None:
            total = total + b
        return total


def solution(mesh):
    ring = Ring(mesh)

    def on_device(queries, keys, values, rates, fast_weights):
        nblocks = queries.shape[0]
        own = fast_weights
        blocks = []
        for span in range(nblocks):
            gathered = ring.gather(own.astype(jnp.bfloat16))
            normed, partial_value = block_step(span, gathered, queries, keys, values, rates)
            blocks.append(normed)
            own = renorm(own, own + ring.reduce(partial_value))
        return (jnp.stack(blocks), own)

    placed = (
        P(None, ("groups", "tok"), None),
        P(None, ("groups", "tok"), None),
        P(None, ("groups", "tok"), None),
        P(None, None, None, ("groups", "tok")),
        P(None, None, "tok", None),
    )
    return jax.shard_map(
        on_device,
        mesh=mesh,
        in_specs=placed,
        out_specs=(P(None, ("groups", "tok"), None), P("groups", None, "tok", None)),
        check_vma=False,
    )
```

```python
import jax
import jax.numpy as jnp
from jax import lax
from jax.sharding import PartitionSpec as P


def cross(left, right):
    return lax.dot_general(
        left, right, (((1,), (1,)), ((), ())), preferred_element_type=jnp.float32
    )


def inner(left, right):
    return lax.dot_general(
        left, right, (((0,), (0,)), ((), ())), preferred_element_type=jnp.float32
    )


def renorm(old, upd):
    old_norm = jnp.sqrt(jnp.mean(old * old, axis=-1))
    new_norm = jnp.sqrt(jnp.mean(upd * upd, axis=-1) + 1e-06)
    return upd * (old_norm / new_norm)[..., None]


def head_step(query, key_rows, value_rows, rate_rows, wbf):
    hidden_q = (jax.nn.silu(cross(query, wbf[0])) * cross(query, wbf[1])).astype(jnp.bfloat16)
    raw = cross(hidden_q, wbf[2])
    normed = (raw / jnp.sqrt(jnp.mean(raw * raw, axis=-1, keepdims=True) + 1e-06)).astype(
        jnp.bfloat16
    )
    h1 = cross(key_rows, wbf[0])
    h3 = cross(key_rows, wbf[1])
    sig = jax.nn.sigmoid(h1)
    act = h1 * sig
    back = jnp.dot(value_rows, wbf[2], preferred_element_type=jnp.float32)
    d1 = back * h3 * sig * (1.0 + h1 * (1.0 - sig))
    d3 = back * act
    e1 = (rate_rows[0][:, None] * d1).astype(jnp.bfloat16)
    e3 = (rate_rows[1][:, None] * d3).astype(jnp.bfloat16)
    b2 = (rate_rows[2][:, None] * (act * h3)).astype(jnp.bfloat16)
    grad = jnp.stack([inner(e1, key_rows), inner(e3, key_rows), inner(value_rows, b2)])
    return (normed, grad)


def block_step(span, gathered, queries, keys, values, rates):
    heads = gathered.shape[0]
    width = gathered.shape[3]
    pieces = []
    grads = []
    for head in range(heads):
        lo = head * width
        normed, grad = head_step(
            queries[span][:, lo : lo + width],
            keys[span][:, lo : lo + width],
            values[span][:, lo : lo + width],
            rates[span][:, head],
            gathered[head],
        )
        pieces.append(normed)
        grads.append(grad)
    return (jnp.concatenate(pieces, axis=1), jnp.stack(grads))


class Ring:
    def __init__(self, mesh):
        tok = mesh.shape["tok"]
        chips = tok // 2
        coords = [tuple(mesh.devices[0, 2 * c].coords) for c in range(chips)]
        ys = sorted({c[1] for c in coords})
        if len(ys) == 2:
            ahead = sorted((c for c in range(chips) if coords[c][1] == ys[0]), key=lambda c: coords[c][2])
            back = sorted((c for c in range(chips) if coords[c][1] == ys[1]), key=lambda c: -coords[c][2])
            cycle = ahead + back
        else:
            cycle = sorted(range(chips), key=lambda c: (coords[c][1], coords[c][2]))
        self.chips = chips
        self.cycle = cycle
        place = [0] * chips
        for i, c in enumerate(cycle):
            place[c] = i
        self.place = place
        self.cw = [(cycle[p] * 2 + k, cycle[(p + 1) % chips] * 2 + k) for p in range(chips) for k in range(2)]
        self.ccw = [(cycle[p] * 2 + k, cycle[(p - 1) % chips] * 2 + k) for p in range(chips) for k in range(2)]
        self.swap = [(t, t ^ 1) for t in range(tok)]
        self.ncw = chips // 2
        self.nccw = chips - 1 - self.ncw

    def chip_at(self, step):
        me = lax.axis_index("tok") // 2
        where = jnp.array(self.place, jnp.int32)[me]
        return jnp.array(self.cycle, jnp.int32)[(where + step) % self.chips]

    def gather(self, own):
        h, g, rows, f = own.shape
        core = lax.axis_index("tok") % 2
        full = jnp.zeros((self.chips, 2, h, g, rows, f), own.dtype)

        def put(full, piece, chip):
            full = lax.dynamic_update_slice(full, piece[None, None], (chip, core, 0, 0, 0, 0))
            other = lax.ppermute(piece, "tok", self.swap)
            return lax.dynamic_update_slice(full, other[None, None], (chip, 1 - core, 0, 0, 0, 0))

        full = put(full, own, lax.axis_index("tok") // 2)
        a = own
        b = own
        for k in range(1, max(self.ncw, self.nccw) + 1):
            if k <= self.ncw:
                a = lax.ppermute(a, "tok", self.cw)
                full = put(full, a, self.chip_at(-k))
            if k <= self.nccw:
                b = lax.ppermute(b, "tok", self.ccw)
                full = put(full, b, self.chip_at(k))
        full = jnp.moveaxis(full, (0, 1), (2, 3))
        return full.reshape(h, g, self.chips * 2 * rows, f)

    def reduce(self, part):
        h, g, r, f = part.shape
        rows = r // (2 * self.chips)
        q = part.reshape(h, g, self.chips, 2, rows, f)
        core = lax.axis_index("tok") % 2

        def chip_sum(step):
            chip = self.chip_at(step)
            keep = lax.dynamic_slice(q, (0, 0, chip, core, 0, 0), (h, g, 1, 1, rows, f))
            send = lax.dynamic_slice(q, (0, 0, chip, 1 - core, 0, 0), (h, g, 1, 1, rows, f))
            got = lax.ppermute(send, "tok", self.swap)
            return (keep + got).reshape(h, g, rows, f)

        total = chip_sum(0)
        a = chip_sum(self.ncw) if self.ncw else None
        b = chip_sum(-self.nccw) if self.nccw else None
        for k in range(1, max(self.ncw, self.nccw) + 1):
            if k <= self.ncw:
                a = lax.ppermute(a.astype(jnp.bfloat16), "tok", self.cw).astype(jnp.float32)
                if k < self.ncw:
                    a = a + chip_sum(self.ncw - k)
            if k <= self.nccw:
                b = lax.ppermute(b.astype(jnp.bfloat16), "tok", self.ccw).astype(jnp.float32)
                if k < self.nccw:
                    b = b + chip_sum(-self.nccw + k)
        if a is not None:
            total = total + a
        if b is not None:
            total = total + b
        return total


def solution(mesh):
    ring = Ring(mesh)

    def on_device(queries, keys, values, rates, fast_weights):
        nblocks = queries.shape[0]
        own = fast_weights
        blocks = []
        heads = own.shape[0]
        width = queries.shape[2] // heads
        if ring.chips > 8:
            for span in range(nblocks):
                gathered = ring.gather(own.astype(jnp.bfloat16))
                normed, partial_value = block_step(span, gathered, queries, keys, values, rates)
                blocks.append(normed)
                own = renorm(own, own + ring.reduce(partial_value))
            return (jnp.stack(blocks), own)
        own = [own[head] for head in range(heads)]
        for span in range(nblocks):
            pieces = []
            for head in range(heads):
                wbf = ring.gather(own[head][None].astype(jnp.bfloat16))[0]
                lo = head * width
                normed, grad = head_step(
                    queries[span][:, lo : lo + width],
                    keys[span][:, lo : lo + width],
                    values[span][:, lo : lo + width],
                    rates[span][:, head],
                    wbf,
                )
                pieces.append(normed)
                own[head] = renorm(own[head], own[head] + ring.reduce(grad[None])[0])
            blocks.append(jnp.concatenate(pieces, axis=1))
        return (jnp.stack(blocks), jnp.stack(own))

    placed = (
        P(None, ("groups", "tok"), None),
        P(None, ("groups", "tok"), None),
        P(None, ("groups", "tok"), None),
        P(None, None, None, ("groups", "tok")),
        P(None, None, "tok", None),
    )
    return jax.shard_map(
        on_device,
        mesh=mesh,
        in_specs=placed,
        out_specs=(P(None, ("groups", "tok"), None), P("groups", None, "tok", None)),
        check_vma=False,
    )
```

```python
import jax
import jax.numpy as jnp
from jax import lax
from jax.sharding import PartitionSpec as P


def cross(left, right):
    return lax.dot_general(
        left, right, (((1,), (1,)), ((), ())), preferred_element_type=jnp.float32
    )


def inner(left, right):
    return lax.dot_general(
        left, right, (((0,), (0,)), ((), ())), preferred_element_type=jnp.float32
    )


def renorm(old, upd):
    old_norm = jnp.sqrt(jnp.mean(old * old, axis=-1))
    new_norm = jnp.sqrt(jnp.mean(upd * upd, axis=-1) + 1e-06)
    return upd * (old_norm / new_norm)[..., None]


def head_step(query, key_rows, value_rows, rate_rows, wbf):
    hidden_q = (jax.nn.silu(cross(query, wbf[0])) * cross(query, wbf[1])).astype(jnp.bfloat16)
    raw = cross(hidden_q, wbf[2])
    normed = (raw / jnp.sqrt(jnp.mean(raw * raw, axis=-1, keepdims=True) + 1e-06)).astype(
        jnp.bfloat16
    )
    h1 = cross(key_rows, wbf[0])
    h3 = cross(key_rows, wbf[1])
    sig = jax.nn.sigmoid(h1)
    act = h1 * sig
    back = jnp.dot(value_rows, wbf[2], preferred_element_type=jnp.float32)
    d1 = back * h3 * sig * (1.0 + h1 * (1.0 - sig))
    d3 = back * act
    e1 = (rate_rows[0][:, None] * d1).astype(jnp.bfloat16)
    e3 = (rate_rows[1][:, None] * d3).astype(jnp.bfloat16)
    b2 = (rate_rows[2][:, None] * (act * h3)).astype(jnp.bfloat16)
    grad = jnp.stack([inner(e1, key_rows), inner(e3, key_rows), inner(value_rows, b2)])
    return (normed, grad)


def block_step(span, gathered, queries, keys, values, rates):
    heads = gathered.shape[0]
    width = gathered.shape[3]
    pieces = []
    grads = []
    for head in range(heads):
        lo = head * width
        normed, grad = head_step(
            queries[span][:, lo : lo + width],
            keys[span][:, lo : lo + width],
            values[span][:, lo : lo + width],
            rates[span][:, head],
            gathered[head],
        )
        pieces.append(normed)
        grads.append(grad)
    return (jnp.concatenate(pieces, axis=1), jnp.stack(grads))


class Ring:
    def __init__(self, mesh):
        tok = mesh.shape["tok"]
        chips = tok // 2
        coords = [tuple(mesh.devices[0, 2 * c].coords) for c in range(chips)]
        ys = sorted({c[1] for c in coords})
        if len(ys) == 2:
            ahead = sorted((c for c in range(chips) if coords[c][1] == ys[0]), key=lambda c: coords[c][2])
            back = sorted((c for c in range(chips) if coords[c][1] == ys[1]), key=lambda c: -coords[c][2])
            cycle = ahead + back
        else:
            cycle = sorted(range(chips), key=lambda c: (coords[c][1], coords[c][2]))
        self.chips = chips
        self.cycle = cycle
        place = [0] * chips
        for i, c in enumerate(cycle):
            place[c] = i
        self.place = place
        self.cw = [(cycle[p] * 2 + k, cycle[(p + 1) % chips] * 2 + k) for p in range(chips) for k in range(2)]
        self.ccw = [(cycle[p] * 2 + k, cycle[(p - 1) % chips] * 2 + k) for p in range(chips) for k in range(2)]
        self.swap = [(t, t ^ 1) for t in range(tok)]
        self.ncw = chips // 2
        self.nccw = chips - 1 - self.ncw

    def chip_at(self, step):
        me = lax.axis_index("tok") // 2
        where = jnp.array(self.place, jnp.int32)[me]
        return jnp.array(self.cycle, jnp.int32)[(where + step) % self.chips]

    def gather(self, own):
        h, g, rows, f = own.shape
        core = lax.axis_index("tok") % 2
        ring = jnp.zeros((self.chips, h, g, rows, f), own.dtype)
        ring = lax.dynamic_update_index_in_dim(ring, own, lax.axis_index("tok") // 2, 0)
        a = own
        b = own
        for k in range(1, max(self.ncw, self.nccw) + 1):
            if k <= self.ncw:
                a = lax.ppermute(a, "tok", self.cw)
                ring = lax.dynamic_update_index_in_dim(ring, a, self.chip_at(-k), 0)
            if k <= self.nccw:
                b = lax.ppermute(b, "tok", self.ccw)
                ring = lax.dynamic_update_index_in_dim(ring, b, self.chip_at(k), 0)
        other = lax.ppermute(ring, "tok", self.swap)
        full = jnp.zeros((self.chips, 2, h, g, rows, f), own.dtype)
        full = lax.dynamic_update_slice(full, ring[:, None], (0, core, 0, 0, 0, 0))
        full = lax.dynamic_update_slice(full, other[:, None], (0, 1 - core, 0, 0, 0, 0))
        full = jnp.moveaxis(full, (0, 1), (2, 3))
        return full.reshape(h, g, self.chips * 2 * rows, f)

    def reduce(self, part):
        h, g, r, f = part.shape
        rows = r // (2 * self.chips)
        q = part.reshape(h, g, self.chips, 2, rows, f)
        core = lax.axis_index("tok") % 2

        def chip_sum(step):
            chip = self.chip_at(step)
            keep = lax.dynamic_slice(q, (0, 0, chip, core, 0, 0), (h, g, 1, 1, rows, f))
            send = lax.dynamic_slice(q, (0, 0, chip, 1 - core, 0, 0), (h, g, 1, 1, rows, f))
            got = lax.ppermute(send, "tok", self.swap)
            return (keep + got).reshape(h, g, rows, f)

        total = chip_sum(0)
        a = chip_sum(self.ncw) if self.ncw else None
        b = chip_sum(-self.nccw) if self.nccw else None
        for k in range(1, max(self.ncw, self.nccw) + 1):
            if k <= self.ncw:
                a = lax.ppermute(a.astype(jnp.bfloat16), "tok", self.cw).astype(jnp.float32)
                if k < self.ncw:
                    a = a + chip_sum(self.ncw - k)
            if k <= self.nccw:
                b = lax.ppermute(b.astype(jnp.bfloat16), "tok", self.ccw).astype(jnp.float32)
                if k < self.nccw:
                    b = b + chip_sum(-self.nccw + k)
        if a is not None:
            total = total + a
        if b is not None:
            total = total + b
        return total


def solution(mesh):
    ring = Ring(mesh)

    def on_device(queries, keys, values, rates, fast_weights):
        nblocks = queries.shape[0]
        own = fast_weights
        blocks = []
        for span in range(nblocks):
            gathered = ring.gather(own.astype(jnp.bfloat16))
            normed, partial_value = block_step(span, gathered, queries, keys, values, rates)
            blocks.append(normed)
            own = renorm(own, own + ring.reduce(partial_value))
        return (jnp.stack(blocks), own)

    placed = (
        P(None, ("groups", "tok"), None),
        P(None, ("groups", "tok"), None),
        P(None, ("groups", "tok"), None),
        P(None, None, None, ("groups", "tok")),
        P(None, None, "tok", None),
    )
    return jax.shard_map(
        on_device,
        mesh=mesh,
        in_specs=placed,
        out_specs=(P(None, ("groups", "tok"), None), P("groups", None, "tok", None)),
        check_vma=False,
    )
```

```python
import jax
import jax.numpy as jnp
from jax import lax
from jax.experimental import pallas as pl
from jax.experimental.pallas import tpu as pltpu
from jax.sharding import PartitionSpec as P


def cross(left, right):
    return lax.dot_general(
        left, right, (((1,), (1,)), ((), ())), preferred_element_type=jnp.float32
    )


def inner(left, right):
    return lax.dot_general(
        left, right, (((0,), (0,)), ((), ())), preferred_element_type=jnp.float32
    )


def renorm(old, upd):
    old_norm = jnp.sqrt(jnp.mean(old * old, axis=-1))
    new_norm = jnp.sqrt(jnp.mean(upd * upd, axis=-1) + 1e-06)
    return upd * (old_norm / new_norm)[..., None]


def head_step(query, key_rows, value_rows, rate_rows, wbf):
    hidden_q = (jax.nn.silu(cross(query, wbf[0])) * cross(query, wbf[1])).astype(jnp.bfloat16)
    raw = cross(hidden_q, wbf[2])
    normed = (raw / jnp.sqrt(jnp.mean(raw * raw, axis=-1, keepdims=True) + 1e-06)).astype(
        jnp.bfloat16
    )
    h1 = cross(key_rows, wbf[0])
    h3 = cross(key_rows, wbf[1])
    sig = jax.nn.sigmoid(h1)
    act = h1 * sig
    back = jnp.dot(value_rows, wbf[2], preferred_element_type=jnp.float32)
    d1 = back * h3 * sig * (1.0 + h1 * (1.0 - sig))
    d3 = back * act
    e1 = (rate_rows[0][:, None] * d1).astype(jnp.bfloat16)
    e3 = (rate_rows[1][:, None] * d3).astype(jnp.bfloat16)
    b2 = (rate_rows[2][:, None] * (act * h3)).astype(jnp.bfloat16)
    grad = jnp.stack([inner(e1, key_rows), inner(e3, key_rows), inner(value_rows, b2)])
    return (normed, grad)


def block_step(span, gathered, queries, keys, values, rates):
    heads = gathered.shape[0]
    width = gathered.shape[3]
    pieces = []
    grads = []
    for head in range(heads):
        lo = head * width
        normed, grad = head_step(
            queries[span][:, lo : lo + width],
            keys[span][:, lo : lo + width],
            values[span][:, lo : lo + width],
            rates[span][:, head],
            gathered[head],
        )
        pieces.append(normed)
        grads.append(grad)
    return (jnp.concatenate(pieces, axis=1), jnp.stack(grads))


def _nt(left, right):
    return lax.dot_general(left, right, (((1,), (1,)), ((), ())), preferred_element_type=jnp.float32)


def _tn(left, right):
    return lax.dot_general(left, right, (((0,), (0,)), ((), ())), preferred_element_type=jnp.float32)


def _block_kernel(q_ref, k_ref, v_ref, r_ref, w_ref, o_ref, g_ref):
    heads = w_ref.shape[0]
    width = w_ref.shape[3]
    for head in range(heads):
        lo = head * width
        query = q_ref[:, lo : lo + width]
        key_rows = k_ref[:, lo : lo + width]
        value_rows = v_ref[:, lo : lo + width]
        gate = w_ref[head, 0]
        up = w_ref[head, 1]
        down = w_ref[head, 2]
        a1 = _nt(query, gate)
        a3 = _nt(query, up)
        hidden_q = (a1 / (1.0 + jnp.exp(-a1)) * a3).astype(jnp.bfloat16)
        raw = _nt(hidden_q, down)
        scale = jnp.sqrt(jnp.mean(raw * raw, axis=-1, keepdims=True) + 1e-06)
        o_ref[:, lo : lo + width] = (raw / scale).astype(jnp.bfloat16)
        h1 = _nt(key_rows, gate)
        h3 = _nt(key_rows, up)
        sig = 1.0 / (1.0 + jnp.exp(-h1))
        act = h1 * sig
        back = jnp.dot(value_rows, down, preferred_element_type=jnp.float32)
        d1 = back * h3 * sig * (1.0 + h1 * (1.0 - sig))
        d3 = back * act
        e1 = (r_ref[:, head : head + 1] * d1).astype(jnp.bfloat16)
        e3 = (r_ref[:, heads + head : heads + head + 1] * d3).astype(jnp.bfloat16)
        b2 = (r_ref[:, 2 * heads + head : 2 * heads + head + 1] * (act * h3)).astype(jnp.bfloat16)
        g_ref[head, 0] = _tn(e1, key_rows)
        g_ref[head, 1] = _tn(e3, key_rows)
        g_ref[head, 2] = _tn(value_rows, b2)


def fused_block(query, key_rows, value_rows, rate_rows, wbf):
    tokens = query.shape[0]
    rates_t = rate_rows.reshape(-1, tokens).T
    return pl.pallas_call(
        _block_kernel,
        out_shape=(
            jax.ShapeDtypeStruct(query.shape, jnp.bfloat16),
            jax.ShapeDtypeStruct(wbf.shape, jnp.float32),
        ),
        compiler_params=pltpu.CompilerParams(vmem_limit_bytes=48 * 1024 * 1024),
    )(query, key_rows, value_rows, rates_t, wbf)


class Ring:
    def __init__(self, mesh):
        tok = mesh.shape["tok"]
        chips = tok // 2
        coords = [tuple(mesh.devices[0, 2 * c].coords) for c in range(chips)]
        ys = sorted({c[1] for c in coords})
        if len(ys) == 2:
            ahead = sorted((c for c in range(chips) if coords[c][1] == ys[0]), key=lambda c: coords[c][2])
            back = sorted((c for c in range(chips) if coords[c][1] == ys[1]), key=lambda c: -coords[c][2])
            cycle = ahead + back
        else:
            cycle = sorted(range(chips), key=lambda c: (coords[c][1], coords[c][2]))
        self.chips = chips
        self.cycle = cycle
        place = [0] * chips
        for i, c in enumerate(cycle):
            place[c] = i
        self.place = place
        self.cw = [(cycle[p] * 2 + k, cycle[(p + 1) % chips] * 2 + k) for p in range(chips) for k in range(2)]
        self.ccw = [(cycle[p] * 2 + k, cycle[(p - 1) % chips] * 2 + k) for p in range(chips) for k in range(2)]
        self.swap = [(t, t ^ 1) for t in range(tok)]
        self.ncw = chips // 2
        self.nccw = chips - 1 - self.ncw

    def chip_at(self, step):
        me = lax.axis_index("tok") // 2
        where = jnp.array(self.place, jnp.int32)[me]
        return jnp.array(self.cycle, jnp.int32)[(where + step) % self.chips]

    def gather(self, own):
        h, g, rows, f = own.shape
        core = lax.axis_index("tok") % 2
        ring = jnp.zeros((self.chips, h, g, rows, f), own.dtype)
        ring = lax.dynamic_update_index_in_dim(ring, own, lax.axis_index("tok") // 2, 0)
        a = own
        b = own
        for k in range(1, max(self.ncw, self.nccw) + 1):
            if k <= self.ncw:
                a = lax.ppermute(a, "tok", self.cw)
                ring = lax.dynamic_update_index_in_dim(ring, a, self.chip_at(-k), 0)
            if k <= self.nccw:
                b = lax.ppermute(b, "tok", self.ccw)
                ring = lax.dynamic_update_index_in_dim(ring, b, self.chip_at(k), 0)
        other = lax.ppermute(ring, "tok", self.swap)
        full = jnp.zeros((self.chips, 2, h, g, rows, f), own.dtype)
        full = lax.dynamic_update_slice(full, ring[:, None], (0, core, 0, 0, 0, 0))
        full = lax.dynamic_update_slice(full, other[:, None], (0, 1 - core, 0, 0, 0, 0))
        full = jnp.moveaxis(full, (0, 1), (2, 3))
        return full.reshape(h, g, self.chips * 2 * rows, f)

    def reduce(self, part):
        h, g, r, f = part.shape
        rows = r // (2 * self.chips)
        q = part.reshape(h, g, self.chips, 2, rows, f)
        core = lax.axis_index("tok") % 2

        def chip_sum(step):
            chip = self.chip_at(step)
            keep = lax.dynamic_slice(q, (0, 0, chip, core, 0, 0), (h, g, 1, 1, rows, f))
            send = lax.dynamic_slice(q, (0, 0, chip, 1 - core, 0, 0), (h, g, 1, 1, rows, f))
            got = lax.ppermute(send, "tok", self.swap)
            return (keep + got).reshape(h, g, rows, f)

        total = chip_sum(0)
        a = chip_sum(self.ncw) if self.ncw else None
        b = chip_sum(-self.nccw) if self.nccw else None
        for k in range(1, max(self.ncw, self.nccw) + 1):
            if k <= self.ncw:
                a = lax.ppermute(a.astype(jnp.bfloat16), "tok", self.cw).astype(jnp.float32)
                if k < self.ncw:
                    a = a + chip_sum(self.ncw - k)
            if k <= self.nccw:
                b = lax.ppermute(b.astype(jnp.bfloat16), "tok", self.ccw).astype(jnp.float32)
                if k < self.nccw:
                    b = b + chip_sum(-self.nccw + k)
        if a is not None:
            total = total + a
        if b is not None:
            total = total + b
        return total


def solution(mesh):
    ring = Ring(mesh)

    def on_device(queries, keys, values, rates, fast_weights):
        nblocks = queries.shape[0]
        own = fast_weights
        blocks = []
        for span in range(nblocks):
            gathered = ring.gather(own.astype(jnp.bfloat16))
            normed, partial_value = fused_block(queries[span], keys[span], values[span], rates[span], gathered)
            blocks.append(normed)
            own = renorm(own, own + ring.reduce(partial_value))
        return (jnp.stack(blocks), own)

    placed = (
        P(None, ("groups", "tok"), None),
        P(None, ("groups", "tok"), None),
        P(None, ("groups", "tok"), None),
        P(None, None, None, ("groups", "tok")),
        P(None, None, "tok", None),
    )
    return jax.shard_map(
        on_device,
        mesh=mesh,
        in_specs=placed,
        out_specs=(P(None, ("groups", "tok"), None), P("groups", None, "tok", None)),
        check_vma=False,
    )
```

```python
import jax
import jax.numpy as jnp
from jax import lax
from jax.experimental import pallas as pl
from jax.experimental.pallas import tpu as pltpu
from jax.sharding import PartitionSpec as P


def cross(left, right):
    return lax.dot_general(
        left, right, (((1,), (1,)), ((), ())), preferred_element_type=jnp.float32
    )


def inner(left, right):
    return lax.dot_general(
        left, right, (((0,), (0,)), ((), ())), preferred_element_type=jnp.float32
    )


def renorm(old, upd):
    old_norm = jnp.sqrt(jnp.mean(old * old, axis=-1))
    new_norm = jnp.sqrt(jnp.mean(upd * upd, axis=-1) + 1e-06)
    return upd * (old_norm / new_norm)[..., None]


def head_step(query, key_rows, value_rows, rate_rows, wbf):
    hidden_q = (jax.nn.silu(cross(query, wbf[0])) * cross(query, wbf[1])).astype(jnp.bfloat16)
    raw = cross(hidden_q, wbf[2])
    normed = (raw / jnp.sqrt(jnp.mean(raw * raw, axis=-1, keepdims=True) + 1e-06)).astype(
        jnp.bfloat16
    )
    h1 = cross(key_rows, wbf[0])
    h3 = cross(key_rows, wbf[1])
    sig = jax.nn.sigmoid(h1)
    act = h1 * sig
    back = jnp.dot(value_rows, wbf[2], preferred_element_type=jnp.float32)
    d1 = back * h3 * sig * (1.0 + h1 * (1.0 - sig))
    d3 = back * act
    e1 = (rate_rows[0][:, None] * d1).astype(jnp.bfloat16)
    e3 = (rate_rows[1][:, None] * d3).astype(jnp.bfloat16)
    b2 = (rate_rows[2][:, None] * (act * h3)).astype(jnp.bfloat16)
    grad = jnp.stack([inner(e1, key_rows), inner(e3, key_rows), inner(value_rows, b2)])
    return (normed, grad)


def block_step(span, gathered, queries, keys, values, rates):
    heads = gathered.shape[0]
    width = gathered.shape[3]
    pieces = []
    grads = []
    for head in range(heads):
        lo = head * width
        normed, grad = head_step(
            queries[span][:, lo : lo + width],
            keys[span][:, lo : lo + width],
            values[span][:, lo : lo + width],
            rates[span][:, head],
            gathered[head],
        )
        pieces.append(normed)
        grads.append(grad)
    return (jnp.concatenate(pieces, axis=1), jnp.stack(grads))


def _nt(left, right):
    return lax.dot_general(left, right, (((1,), (1,)), ((), ())), preferred_element_type=jnp.float32)


def _tn(left, right):
    return lax.dot_general(left, right, (((0,), (0,)), ((), ())), preferred_element_type=jnp.float32)


def _block_kernel(q_ref, k_ref, v_ref, r_ref, w_ref, o_ref, g_ref):
    heads = w_ref.shape[0]
    width = w_ref.shape[3]
    for head in range(heads):
        lo = head * width
        query = q_ref[:, lo : lo + width]
        key_rows = k_ref[:, lo : lo + width]
        value_rows = v_ref[:, lo : lo + width]
        gate = w_ref[head, 0]
        up = w_ref[head, 1]
        down = w_ref[head, 2]
        a1 = _nt(query, gate)
        a3 = _nt(query, up)
        hidden_q = (a1 / (1.0 + jnp.exp(-a1)) * a3).astype(jnp.bfloat16)
        raw = _nt(hidden_q, down)
        scale = jnp.sqrt(jnp.mean(raw * raw, axis=-1, keepdims=True) + 1e-06)
        o_ref[:, lo : lo + width] = (raw / scale).astype(jnp.bfloat16)
        h1 = _nt(key_rows, gate)
        h3 = _nt(key_rows, up)
        sig = 1.0 / (1.0 + jnp.exp(-h1))
        act = h1 * sig
        back = jnp.dot(value_rows, down, preferred_element_type=jnp.float32)
        d1 = back * h3 * sig * (1.0 + h1 * (1.0 - sig))
        d3 = back * act
        e1 = (r_ref[:, head : head + 1] * d1).astype(jnp.bfloat16)
        e3 = (r_ref[:, heads + head : heads + head + 1] * d3).astype(jnp.bfloat16)
        b2 = (r_ref[:, 2 * heads + head : 2 * heads + head + 1] * (act * h3)).astype(jnp.bfloat16)
        g_ref[head, 0] = _tn(e1, key_rows)
        g_ref[head, 1] = _tn(e3, key_rows)
        g_ref[head, 2] = _tn(value_rows, b2)


def fused_block(query, key_rows, value_rows, rate_rows, wbf):
    tokens = query.shape[0]
    rates_t = rate_rows.reshape(-1, tokens).T
    return pl.pallas_call(
        _block_kernel,
        out_shape=(
            jax.ShapeDtypeStruct(query.shape, jnp.bfloat16),
            jax.ShapeDtypeStruct(wbf.shape, jnp.float32),
        ),
        compiler_params=pltpu.CompilerParams(vmem_limit_bytes=48 * 1024 * 1024),
    )(query, key_rows, value_rows, rates_t, wbf)


class Ring:
    def __init__(self, mesh):
        tok = mesh.shape["tok"]
        chips = tok // 2
        coords = [tuple(mesh.devices[0, 2 * c].coords) for c in range(chips)]
        ys = sorted({c[1] for c in coords})
        if len(ys) == 2:
            ahead = sorted((c for c in range(chips) if coords[c][1] == ys[0]), key=lambda c: coords[c][2])
            back = sorted((c for c in range(chips) if coords[c][1] == ys[1]), key=lambda c: -coords[c][2])
            cycle = ahead + back
        else:
            cycle = sorted(range(chips), key=lambda c: (coords[c][1], coords[c][2]))
        self.chips = chips
        self.cycle = cycle
        place = [0] * chips
        for i, c in enumerate(cycle):
            place[c] = i
        self.place = place
        self.cw = [(cycle[p] * 2 + k, cycle[(p + 1) % chips] * 2 + k) for p in range(chips) for k in range(2)]
        self.ccw = [(cycle[p] * 2 + k, cycle[(p - 1) % chips] * 2 + k) for p in range(chips) for k in range(2)]
        self.swap = [(t, t ^ 1) for t in range(tok)]
        self.ncw = chips // 2
        self.nccw = chips - 1 - self.ncw

    def chip_at(self, step):
        me = lax.axis_index("tok") // 2
        where = jnp.array(self.place, jnp.int32)[me]
        return jnp.array(self.cycle, jnp.int32)[(where + step) % self.chips]

    def offset_table(self):
        return [[(self.place[c] - self.place[t // 2]) % self.chips for c in range(self.chips)] for t in range(2 * self.chips)]

    def gather(self, own):
        h, g, rows, f = own.shape
        chips = self.chips
        me = lax.axis_index("tok")
        core = me % 2
        by_offset = [own] + [None] * (chips - 1)
        a = own
        b = own
        for k in range(1, max(self.ncw, self.nccw) + 1):
            if k <= self.ncw:
                a = lax.ppermute(a, "tok", self.cw)
                by_offset[chips - k] = a
            if k <= self.nccw:
                b = lax.ppermute(b, "tok", self.ccw)
                by_offset[k] = b
        mine = jnp.stack(by_offset)
        other = lax.ppermute(mine, "tok", self.swap)
        both = jnp.concatenate([mine, other], axis=0)
        offsets = jnp.array(self.offset_table(), jnp.int32)[me]
        pick = jnp.stack([offsets + chips * core, offsets + chips * (1 - core)], axis=1).reshape(-1)
        full = jnp.take(both, pick, axis=0)
        full = full.reshape(chips, 2, h, g, rows, f)
        full = jnp.moveaxis(full, (0, 1), (2, 3))
        return full.reshape(h, g, chips * 2 * rows, f)

    def reduce(self, part):
        h, g, r, f = part.shape
        rows = r // (2 * self.chips)
        q = part.reshape(h, g, self.chips, 2, rows, f)
        core = lax.axis_index("tok") % 2
        need = []
        for k in range(max(self.ncw, self.nccw)):
            if k < self.ncw:
                need.append(self.ncw - k)
            if k < self.nccw:
                need.append(k - self.nccw)
        need.append(0)
        batches = [need[:2], need[2:4], need[4:]]
        sums = {}
        for batch in batches:
            if not batch:
                continue
            chips = [self.chip_at(j) for j in batch]
            keep = jnp.stack([lax.dynamic_slice(q, (0, 0, c, core, 0, 0), (h, g, 1, 1, rows, f)) for c in chips])
            send = jnp.stack([lax.dynamic_slice(q, (0, 0, c, 1 - core, 0, 0), (h, g, 1, 1, rows, f)) for c in chips])
            total = keep + lax.ppermute(send, "tok", self.swap)
            for i, j in enumerate(batch):
                sums[j] = total[i].reshape(h, g, rows, f)
        out = sums[0]
        a = sums[self.ncw] if self.ncw else None
        b = sums[-self.nccw] if self.nccw else None
        for k in range(1, max(self.ncw, self.nccw) + 1):
            if k <= self.ncw:
                a = lax.ppermute(a.astype(jnp.bfloat16), "tok", self.cw).astype(jnp.float32)
                if k < self.ncw:
                    a = a + sums[self.ncw - k]
            if k <= self.nccw:
                b = lax.ppermute(b.astype(jnp.bfloat16), "tok", self.ccw).astype(jnp.float32)
                if k < self.nccw:
                    b = b + sums[-self.nccw + k]
        if a is not None:
            out = out + a
        if b is not None:
            out = out + b
        return out


def solution(mesh):
    ring = Ring(mesh)

    def on_device(queries, keys, values, rates, fast_weights):
        nblocks = queries.shape[0]
        own = fast_weights
        blocks = []
        for span in range(nblocks):
            gathered = ring.gather(own.astype(jnp.bfloat16))
            normed, partial_value = fused_block(queries[span], keys[span], values[span], rates[span], gathered)
            blocks.append(normed)
            own = renorm(own, own + ring.reduce(partial_value))
        return (jnp.stack(blocks), own)

    placed = (
        P(None, ("groups", "tok"), None),
        P(None, ("groups", "tok"), None),
        P(None, ("groups", "tok"), None),
        P(None, None, None, ("groups", "tok")),
        P(None, None, "tok", None),
    )
    return jax.shard_map(
        on_device,
        mesh=mesh,
        in_specs=placed,
        out_specs=(P(None, ("groups", "tok"), None), P("groups", None, "tok", None)),
        check_vma=False,
    )
```

```python
import jax
import jax.numpy as jnp
from jax import lax
from jax.experimental import pallas as pl
from jax.experimental.pallas import tpu as pltpu
from jax.sharding import PartitionSpec as P


def cross(left, right):
    return lax.dot_general(
        left, right, (((1,), (1,)), ((), ())), preferred_element_type=jnp.float32
    )


def inner(left, right):
    return lax.dot_general(
        left, right, (((0,), (0,)), ((), ())), preferred_element_type=jnp.float32
    )


def renorm(old, upd):
    old_norm = jnp.sqrt(jnp.mean(old * old, axis=-1))
    new_norm = jnp.sqrt(jnp.mean(upd * upd, axis=-1) + 1e-06)
    return upd * (old_norm / new_norm)[..., None]


def head_step(query, key_rows, value_rows, rate_rows, wbf):
    hidden_q = (jax.nn.silu(cross(query, wbf[0])) * cross(query, wbf[1])).astype(jnp.bfloat16)
    raw = cross(hidden_q, wbf[2])
    normed = (raw / jnp.sqrt(jnp.mean(raw * raw, axis=-1, keepdims=True) + 1e-06)).astype(
        jnp.bfloat16
    )
    h1 = cross(key_rows, wbf[0])
    h3 = cross(key_rows, wbf[1])
    sig = jax.nn.sigmoid(h1)
    act = h1 * sig
    back = jnp.dot(value_rows, wbf[2], preferred_element_type=jnp.float32)
    d1 = back * h3 * sig * (1.0 + h1 * (1.0 - sig))
    d3 = back * act
    e1 = (rate_rows[0][:, None] * d1).astype(jnp.bfloat16)
    e3 = (rate_rows[1][:, None] * d3).astype(jnp.bfloat16)
    b2 = (rate_rows[2][:, None] * (act * h3)).astype(jnp.bfloat16)
    grad = jnp.stack([inner(e1, key_rows), inner(e3, key_rows), inner(value_rows, b2)])
    return (normed, grad)


def block_step(span, gathered, queries, keys, values, rates):
    heads = gathered.shape[0]
    width = gathered.shape[3]
    pieces = []
    grads = []
    for head in range(heads):
        lo = head * width
        normed, grad = head_step(
            queries[span][:, lo : lo + width],
            keys[span][:, lo : lo + width],
            values[span][:, lo : lo + width],
            rates[span][:, head],
            gathered[head],
        )
        pieces.append(normed)
        grads.append(grad)
    return (jnp.concatenate(pieces, axis=1), jnp.stack(grads))


def _nt(left, right):
    return lax.dot_general(left, right, (((1,), (1,)), ((), ())), preferred_element_type=jnp.float32)


def _tn(left, right):
    return lax.dot_general(left, right, (((0,), (0,)), ((), ())), preferred_element_type=jnp.float32)


def _block_kernel(q_ref, k_ref, v_ref, r_ref, w_ref, o_ref, g_ref):
    heads = w_ref.shape[0]
    width = w_ref.shape[3]
    for head in range(heads):
        lo = head * width
        query = q_ref[:, lo : lo + width]
        key_rows = k_ref[:, lo : lo + width]
        value_rows = v_ref[:, lo : lo + width]
        gate = w_ref[head, 0]
        up = w_ref[head, 1]
        down = w_ref[head, 2]
        a1 = _nt(query, gate)
        a3 = _nt(query, up)
        hidden_q = (a1 / (1.0 + jnp.exp(-a1)) * a3).astype(jnp.bfloat16)
        raw = _nt(hidden_q, down)
        scale = jnp.sqrt(jnp.mean(raw * raw, axis=-1, keepdims=True) + 1e-06)
        o_ref[:, lo : lo + width] = (raw / scale).astype(jnp.bfloat16)
        h1 = _nt(key_rows, gate)
        h3 = _nt(key_rows, up)
        sig = 1.0 / (1.0 + jnp.exp(-h1))
        act = h1 * sig
        back = jnp.dot(value_rows, down, preferred_element_type=jnp.float32)
        d1 = back * h3 * sig * (1.0 + h1 * (1.0 - sig))
        d3 = back * act
        e1 = (r_ref[:, head : head + 1] * d1).astype(jnp.bfloat16)
        e3 = (r_ref[:, heads + head : heads + head + 1] * d3).astype(jnp.bfloat16)
        b2 = (r_ref[:, 2 * heads + head : 2 * heads + head + 1] * (act * h3)).astype(jnp.bfloat16)
        chips = g_ref.shape[0]
        rows = g_ref.shape[4]
        for which, grad in enumerate((_tn(e1, key_rows), _tn(e3, key_rows), _tn(value_rows, b2))):
            for chip in range(chips):
                for core in range(2):
                    lo_row = (2 * chip + core) * rows
                    g_ref[chip, core, head, which] = grad[lo_row : lo_row + rows]


def fused_block(query, key_rows, value_rows, rate_rows, wbf, chips):
    tokens = query.shape[0]
    rates_t = rate_rows.reshape(-1, tokens).T
    heads, mats, hid, dh = wbf.shape
    return pl.pallas_call(
        _block_kernel,
        out_shape=(
            jax.ShapeDtypeStruct(query.shape, jnp.bfloat16),
            jax.ShapeDtypeStruct((chips, 2, heads, mats, hid // (2 * chips), dh), jnp.float32),
        ),
        compiler_params=pltpu.CompilerParams(vmem_limit_bytes=48 * 1024 * 1024),
    )(query, key_rows, value_rows, rates_t, wbf)


class Ring:
    def __init__(self, mesh):
        tok = mesh.shape["tok"]
        chips = tok // 2
        coords = [tuple(mesh.devices[0, 2 * c].coords) for c in range(chips)]
        ys = sorted({c[1] for c in coords})
        if len(ys) == 2:
            ahead = sorted((c for c in range(chips) if coords[c][1] == ys[0]), key=lambda c: coords[c][2])
            back = sorted((c for c in range(chips) if coords[c][1] == ys[1]), key=lambda c: -coords[c][2])
            cycle = ahead + back
        else:
            cycle = sorted(range(chips), key=lambda c: (coords[c][1], coords[c][2]))
        self.chips = chips
        self.cycle = cycle
        place = [0] * chips
        for i, c in enumerate(cycle):
            place[c] = i
        self.place = place
        self.cw = [(cycle[p] * 2 + k, cycle[(p + 1) % chips] * 2 + k) for p in range(chips) for k in range(2)]
        self.ccw = [(cycle[p] * 2 + k, cycle[(p - 1) % chips] * 2 + k) for p in range(chips) for k in range(2)]
        self.swap = [(t, t ^ 1) for t in range(tok)]
        self.ncw = chips // 2
        self.nccw = chips - 1 - self.ncw

    def chip_at(self, step):
        me = lax.axis_index("tok") // 2
        where = jnp.array(self.place, jnp.int32)[me]
        return jnp.array(self.cycle, jnp.int32)[(where + step) % self.chips]

    def gather(self, own):
        h, g, rows, f = own.shape
        core = lax.axis_index("tok") % 2
        ring = jnp.zeros((self.chips, h, g, rows, f), own.dtype)
        ring = lax.dynamic_update_index_in_dim(ring, own, lax.axis_index("tok") // 2, 0)
        a = own
        b = own
        for k in range(1, max(self.ncw, self.nccw) + 1):
            if k <= self.ncw:
                a = lax.ppermute(a, "tok", self.cw)
                ring = lax.dynamic_update_index_in_dim(ring, a, self.chip_at(-k), 0)
            if k <= self.nccw:
                b = lax.ppermute(b, "tok", self.ccw)
                ring = lax.dynamic_update_index_in_dim(ring, b, self.chip_at(k), 0)
        other = lax.ppermute(ring, "tok", self.swap)
        full = jnp.zeros((self.chips, 2, h, g, rows, f), own.dtype)
        full = lax.dynamic_update_slice(full, ring[:, None], (0, core, 0, 0, 0, 0))
        full = lax.dynamic_update_slice(full, other[:, None], (0, 1 - core, 0, 0, 0, 0))
        full = jnp.moveaxis(full, (0, 1), (2, 3))
        return full.reshape(h, g, self.chips * 2 * rows, f)

    def reduce(self, q):
        _, _, h, g, rows, f = q.shape
        core = lax.axis_index("tok") % 2

        def chip_sum(step):
            chip = self.chip_at(step)
            keep = lax.dynamic_slice(q, (chip, core, 0, 0, 0, 0), (1, 1, h, g, rows, f))
            send = lax.dynamic_slice(q, (chip, 1 - core, 0, 0, 0, 0), (1, 1, h, g, rows, f))
            got = lax.ppermute(send, "tok", self.swap)
            return (keep + got).reshape(h, g, rows, f)

        total = chip_sum(0)
        a = chip_sum(self.ncw) if self.ncw else None
        b = chip_sum(-self.nccw) if self.nccw else None
        for k in range(1, max(self.ncw, self.nccw) + 1):
            if k <= self.ncw:
                a = lax.ppermute(a.astype(jnp.bfloat16), "tok", self.cw).astype(jnp.float32)
                if k < self.ncw:
                    a = a + chip_sum(self.ncw - k)
            if k <= self.nccw:
                b = lax.ppermute(b.astype(jnp.bfloat16), "tok", self.ccw).astype(jnp.float32)
                if k < self.nccw:
                    b = b + chip_sum(-self.nccw + k)
        if a is not None:
            total = total + a
        if b is not None:
            total = total + b
        return total


def solution(mesh):
    ring = Ring(mesh)

    def on_device(queries, keys, values, rates, fast_weights):
        nblocks = queries.shape[0]
        own = fast_weights
        blocks = []
        for span in range(nblocks):
            gathered = ring.gather(own.astype(jnp.bfloat16))
            normed, partial_value = fused_block(queries[span], keys[span], values[span], rates[span], gathered, ring.chips)
            blocks.append(normed)
            own = renorm(own, own + ring.reduce(partial_value))
        return (jnp.stack(blocks), own)

    placed = (
        P(None, ("groups", "tok"), None),
        P(None, ("groups", "tok"), None),
        P(None, ("groups", "tok"), None),
        P(None, None, None, ("groups", "tok")),
        P(None, None, "tok", None),
    )
    return jax.shard_map(
        on_device,
        mesh=mesh,
        in_specs=placed,
        out_specs=(P(None, ("groups", "tok"), None), P("groups", None, "tok", None)),
        check_vma=False,
    )
```

```python
import jax
import jax.numpy as jnp
from jax import lax
from jax.experimental import pallas as pl
from jax.experimental.pallas import tpu as pltpu
from jax.sharding import PartitionSpec as P


def cross(left, right):
    return lax.dot_general(
        left, right, (((1,), (1,)), ((), ())), preferred_element_type=jnp.float32
    )


def inner(left, right):
    return lax.dot_general(
        left, right, (((0,), (0,)), ((), ())), preferred_element_type=jnp.float32
    )


def renorm(old, upd):
    old_norm = jnp.sqrt(jnp.mean(old * old, axis=-1))
    new_norm = jnp.sqrt(jnp.mean(upd * upd, axis=-1) + 1e-06)
    return upd * (old_norm / new_norm)[..., None]


def head_step(query, key_rows, value_rows, rate_rows, wbf):
    hidden_q = (jax.nn.silu(cross(query, wbf[0])) * cross(query, wbf[1])).astype(jnp.bfloat16)
    raw = cross(hidden_q, wbf[2])
    normed = (raw / jnp.sqrt(jnp.mean(raw * raw, axis=-1, keepdims=True) + 1e-06)).astype(
        jnp.bfloat16
    )
    h1 = cross(key_rows, wbf[0])
    h3 = cross(key_rows, wbf[1])
    sig = jax.nn.sigmoid(h1)
    act = h1 * sig
    back = jnp.dot(value_rows, wbf[2], preferred_element_type=jnp.float32)
    d1 = back * h3 * sig * (1.0 + h1 * (1.0 - sig))
    d3 = back * act
    e1 = (rate_rows[0][:, None] * d1).astype(jnp.bfloat16)
    e3 = (rate_rows[1][:, None] * d3).astype(jnp.bfloat16)
    b2 = (rate_rows[2][:, None] * (act * h3)).astype(jnp.bfloat16)
    grad = jnp.stack([inner(e1, key_rows), inner(e3, key_rows), inner(value_rows, b2)])
    return (normed, grad)


def block_step(span, gathered, queries, keys, values, rates):
    heads = gathered.shape[0]
    width = gathered.shape[3]
    pieces = []
    grads = []
    for head in range(heads):
        lo = head * width
        normed, grad = head_step(
            queries[span][:, lo : lo + width],
            keys[span][:, lo : lo + width],
            values[span][:, lo : lo + width],
            rates[span][:, head],
            gathered[head],
        )
        pieces.append(normed)
        grads.append(grad)
    return (jnp.concatenate(pieces, axis=1), jnp.stack(grads))


def _nt(left, right):
    return lax.dot_general(left, right, (((1,), (1,)), ((), ())), preferred_element_type=jnp.float32)


def _tn(left, right):
    return lax.dot_general(left, right, (((0,), (0,)), ((), ())), preferred_element_type=jnp.float32)


def _block_kernel(q_ref, k_ref, v_ref, r_ref, w_ref, o_ref, g_ref):
    heads = w_ref.shape[0]
    width = w_ref.shape[3]
    for head in range(heads):
        lo = head * width
        query = q_ref[:, lo : lo + width]
        key_rows = k_ref[:, lo : lo + width]
        value_rows = v_ref[:, lo : lo + width]
        gate = w_ref[head, 0]
        up = w_ref[head, 1]
        down = w_ref[head, 2]
        a1 = _nt(query, gate)
        a3 = _nt(query, up)
        hidden_q = (a1 / (1.0 + jnp.exp(-a1)) * a3).astype(jnp.bfloat16)
        raw = _nt(hidden_q, down)
        scale = jnp.sqrt(jnp.mean(raw * raw, axis=-1, keepdims=True) + 1e-06)
        o_ref[:, lo : lo + width] = (raw / scale).astype(jnp.bfloat16)
        h1 = _nt(key_rows, gate)
        h3 = _nt(key_rows, up)
        sig = 1.0 / (1.0 + jnp.exp(-h1))
        act = h1 * sig
        back = jnp.dot(value_rows, down, preferred_element_type=jnp.float32)
        d1 = back * h3 * sig * (1.0 + h1 * (1.0 - sig))
        d3 = back * act
        e1 = (r_ref[:, head : head + 1] * d1).astype(jnp.bfloat16)
        e3 = (r_ref[:, heads + head : heads + head + 1] * d3).astype(jnp.bfloat16)
        b2 = (r_ref[:, 2 * heads + head : 2 * heads + head + 1] * (act * h3)).astype(jnp.bfloat16)
        chips = g_ref.shape[0]
        rows = g_ref.shape[4]
        for which, grad in enumerate((_tn(e1, key_rows), _tn(e3, key_rows), _tn(value_rows, b2))):
            for chip in range(chips):
                for core in range(2):
                    lo_row = (2 * chip + core) * rows
                    g_ref[chip, core, head, which] = grad[lo_row : lo_row + rows]


def fused_block(query, key_rows, value_rows, rate_rows, wbf, chips):
    tokens = query.shape[0]
    rates_t = rate_rows.reshape(-1, tokens).T
    heads, mats, hid, dh = wbf.shape
    return pl.pallas_call(
        _block_kernel,
        out_shape=(
            jax.ShapeDtypeStruct(query.shape, jnp.bfloat16),
            jax.ShapeDtypeStruct((chips, 2, heads, mats, hid // (2 * chips), dh), jnp.float32),
        ),
        compiler_params=pltpu.CompilerParams(vmem_limit_bytes=48 * 1024 * 1024),
    )(query, key_rows, value_rows, rates_t, wbf)


class Ring:
    def __init__(self, mesh):
        tok = mesh.shape["tok"]
        chips = tok // 2
        coords = [tuple(mesh.devices[0, 2 * c].coords) for c in range(chips)]
        ys = sorted({c[1] for c in coords})
        if len(ys) == 2:
            ahead = sorted((c for c in range(chips) if coords[c][1] == ys[0]), key=lambda c: coords[c][2])
            back = sorted((c for c in range(chips) if coords[c][1] == ys[1]), key=lambda c: -coords[c][2])
            cycle = ahead + back
        else:
            cycle = sorted(range(chips), key=lambda c: (coords[c][1], coords[c][2]))
        self.chips = chips
        self.cycle = cycle
        place = [0] * chips
        for i, c in enumerate(cycle):
            place[c] = i
        self.place = place
        self.cw = [(cycle[p] * 2 + k, cycle[(p + 1) % chips] * 2 + k) for p in range(chips) for k in range(2)]
        self.ccw = [(cycle[p] * 2 + k, cycle[(p - 1) % chips] * 2 + k) for p in range(chips) for k in range(2)]
        self.swap = [(t, t ^ 1) for t in range(tok)]
        self.ncw = chips // 2
        self.nccw = chips - 1 - self.ncw

    def chip_at(self, step):
        me = lax.axis_index("tok") // 2
        where = jnp.array(self.place, jnp.int32)[me]
        return jnp.array(self.cycle, jnp.int32)[(where + step) % self.chips]

    def gather(self, own):
        h, g, rows, f = own.shape
        core = lax.axis_index("tok") % 2
        even = self.chips % 2 == 0
        ring = jnp.zeros((self.chips, h, g, rows, f), own.dtype)
        ring = lax.dynamic_update_index_in_dim(ring, own, lax.axis_index("tok") // 2, 0)
        a = own
        b = own
        last = self.ncw if even else 0
        for k in range(1, max(self.ncw, self.nccw) + 1):
            if k == last:
                a = lax.ppermute(a[..., : f // 2], "tok", self.cw)
                b = lax.ppermute(b[..., f // 2 :], "tok", self.ccw)
                ring = lax.dynamic_update_index_in_dim(ring, jnp.concatenate([a, b], -1), self.chip_at(k), 0)
                continue
            if k <= self.ncw:
                a = lax.ppermute(a, "tok", self.cw)
                ring = lax.dynamic_update_index_in_dim(ring, a, self.chip_at(-k), 0)
            if k <= self.nccw:
                b = lax.ppermute(b, "tok", self.ccw)
                ring = lax.dynamic_update_index_in_dim(ring, b, self.chip_at(k), 0)
        other = lax.ppermute(ring, "tok", self.swap)
        full = jnp.zeros((self.chips, 2, h, g, rows, f), own.dtype)
        full = lax.dynamic_update_slice(full, ring[:, None], (0, core, 0, 0, 0, 0))
        full = lax.dynamic_update_slice(full, other[:, None], (0, 1 - core, 0, 0, 0, 0))
        full = jnp.moveaxis(full, (0, 1), (2, 3))
        return full.reshape(h, g, self.chips * 2 * rows, f)

    def reduce(self, q):
        _, _, h, g, rows, f = q.shape
        core = lax.axis_index("tok") % 2

        def chip_sum(step):
            chip = self.chip_at(step)
            keep = lax.dynamic_slice(q, (chip, core, 0, 0, 0, 0), (1, 1, h, g, rows, f))
            send = lax.dynamic_slice(q, (chip, 1 - core, 0, 0, 0, 0), (1, 1, h, g, rows, f))
            got = lax.ppermute(send, "tok", self.swap)
            return (keep + got).reshape(h, g, rows, f)

        total = chip_sum(0)
        if self.chips % 2 == 0:
            n = self.chips // 2
            half = f // 2
            far = chip_sum(n)
            a = far[..., :half]
            b = far[..., half:]
            for k in range(1, n + 1):
                a = lax.ppermute(a.astype(jnp.bfloat16), "tok", self.cw).astype(jnp.float32)
                b = lax.ppermute(b.astype(jnp.bfloat16), "tok", self.ccw).astype(jnp.float32)
                if k < n:
                    near_a = chip_sum(n - k)
                    near_b = chip_sum(k - n)
                    if k == 1:
                        a = jnp.concatenate([a + near_a[..., :half], near_a[..., half:]], -1)
                        b = jnp.concatenate([near_b[..., :half], b + near_b[..., half:]], -1)
                    else:
                        a = a + near_a
                        b = b + near_b
            if n == 1:
                return total + jnp.concatenate([a, b], -1)
            return total + a + b
        a = chip_sum(self.ncw) if self.ncw else None
        b = chip_sum(-self.nccw) if self.nccw else None
        for k in range(1, max(self.ncw, self.nccw) + 1):
            if k <= self.ncw:
                a = lax.ppermute(a.astype(jnp.bfloat16), "tok", self.cw).astype(jnp.float32)
                if k < self.ncw:
                    a = a + chip_sum(self.ncw - k)
            if k <= self.nccw:
                b = lax.ppermute(b.astype(jnp.bfloat16), "tok", self.ccw).astype(jnp.float32)
                if k < self.nccw:
                    b = b + chip_sum(-self.nccw + k)
        if a is not None:
            total = total + a
        if b is not None:
            total = total + b
        return total


def solution(mesh):
    ring = Ring(mesh)

    def on_device(queries, keys, values, rates, fast_weights):
        nblocks = queries.shape[0]
        own = fast_weights
        blocks = []
        for span in range(nblocks):
            gathered = ring.gather(own.astype(jnp.bfloat16))
            normed, partial_value = fused_block(queries[span], keys[span], values[span], rates[span], gathered, ring.chips)
            blocks.append(normed)
            own = renorm(own, own + ring.reduce(partial_value))
        return (jnp.stack(blocks), own)

    placed = (
        P(None, ("groups", "tok"), None),
        P(None, ("groups", "tok"), None),
        P(None, ("groups", "tok"), None),
        P(None, None, None, ("groups", "tok")),
        P(None, None, "tok", None),
    )
    return jax.shard_map(
        on_device,
        mesh=mesh,
        in_specs=placed,
        out_specs=(P(None, ("groups", "tok"), None), P("groups", None, "tok", None)),
        check_vma=False,
    )
```

```python
import jax
import jax.numpy as jnp
from jax import lax
from jax.experimental import pallas as pl
from jax.experimental.pallas import tpu as pltpu
from jax.sharding import PartitionSpec as P


def cross(left, right):
    return lax.dot_general(
        left, right, (((1,), (1,)), ((), ())), preferred_element_type=jnp.float32
    )


def inner(left, right):
    return lax.dot_general(
        left, right, (((0,), (0,)), ((), ())), preferred_element_type=jnp.float32
    )


def renorm(old, upd):
    old_norm = jnp.sqrt(jnp.mean(old * old, axis=-1))
    new_norm = jnp.sqrt(jnp.mean(upd * upd, axis=-1) + 1e-06)
    return upd * (old_norm / new_norm)[..., None]


def head_step(query, key_rows, value_rows, rate_rows, wbf):
    hidden_q = (jax.nn.silu(cross(query, wbf[0])) * cross(query, wbf[1])).astype(jnp.bfloat16)
    raw = cross(hidden_q, wbf[2])
    normed = (raw / jnp.sqrt(jnp.mean(raw * raw, axis=-1, keepdims=True) + 1e-06)).astype(
        jnp.bfloat16
    )
    h1 = cross(key_rows, wbf[0])
    h3 = cross(key_rows, wbf[1])
    sig = jax.nn.sigmoid(h1)
    act = h1 * sig
    back = jnp.dot(value_rows, wbf[2], preferred_element_type=jnp.float32)
    d1 = back * h3 * sig * (1.0 + h1 * (1.0 - sig))
    d3 = back * act
    e1 = (rate_rows[0][:, None] * d1).astype(jnp.bfloat16)
    e3 = (rate_rows[1][:, None] * d3).astype(jnp.bfloat16)
    b2 = (rate_rows[2][:, None] * (act * h3)).astype(jnp.bfloat16)
    grad = jnp.stack([inner(e1, key_rows), inner(e3, key_rows), inner(value_rows, b2)])
    return (normed, grad)


def block_step(span, gathered, queries, keys, values, rates):
    heads = gathered.shape[0]
    width = gathered.shape[3]
    pieces = []
    grads = []
    for head in range(heads):
        lo = head * width
        normed, grad = head_step(
            queries[span][:, lo : lo + width],
            keys[span][:, lo : lo + width],
            values[span][:, lo : lo + width],
            rates[span][:, head],
            gathered[head],
        )
        pieces.append(normed)
        grads.append(grad)
    return (jnp.concatenate(pieces, axis=1), jnp.stack(grads))


def _nt(left, right):
    return lax.dot_general(left, right, (((1,), (1,)), ((), ())), preferred_element_type=jnp.float32)


def _tn(left, right):
    return lax.dot_general(left, right, (((0,), (0,)), ((), ())), preferred_element_type=jnp.float32)


def _block_kernel(core_ref, q_ref, k_ref, v_ref, r_ref, mine_ref, other_ref, o_ref, g_ref, w_ref):
    chips, heads, mats, rows, width = mine_ref.shape
    first = core_ref[0] == 0
    for chip in range(chips):
        for head in range(heads):
            for which in range(mats):
                mine = mine_ref[chip, head, which].astype(jnp.float32)
                other = other_ref[chip, head, which].astype(jnp.float32)
                lo_row = 2 * chip * rows
                w_ref[head, which, lo_row : lo_row + rows] = jnp.where(first, mine, other)
                w_ref[head, which, lo_row + rows : lo_row + 2 * rows] = jnp.where(first, other, mine)
    for head in range(heads):
        lo = head * width
        query = q_ref[:, lo : lo + width]
        key_rows = k_ref[:, lo : lo + width]
        value_rows = v_ref[:, lo : lo + width]
        gate = w_ref[head, 0].astype(jnp.bfloat16)
        up = w_ref[head, 1].astype(jnp.bfloat16)
        down = w_ref[head, 2].astype(jnp.bfloat16)
        a1 = _nt(query, gate)
        a3 = _nt(query, up)
        hidden_q = (a1 / (1.0 + jnp.exp(-a1)) * a3).astype(jnp.bfloat16)
        raw = _nt(hidden_q, down)
        scale = jnp.sqrt(jnp.mean(raw * raw, axis=-1, keepdims=True) + 1e-06)
        o_ref[:, lo : lo + width] = (raw / scale).astype(jnp.bfloat16)
        h1 = _nt(key_rows, gate)
        h3 = _nt(key_rows, up)
        sig = 1.0 / (1.0 + jnp.exp(-h1))
        act = h1 * sig
        back = jnp.dot(value_rows, down, preferred_element_type=jnp.float32)
        d1 = back * h3 * sig * (1.0 + h1 * (1.0 - sig))
        d3 = back * act
        e1 = (r_ref[:, head : head + 1] * d1).astype(jnp.bfloat16)
        e3 = (r_ref[:, heads + head : heads + head + 1] * d3).astype(jnp.bfloat16)
        b2 = (r_ref[:, 2 * heads + head : 2 * heads + head + 1] * (act * h3)).astype(jnp.bfloat16)
        chips = g_ref.shape[0]
        rows = g_ref.shape[4]
        for which, grad in enumerate((_tn(e1, key_rows), _tn(e3, key_rows), _tn(value_rows, b2))):
            for chip in range(chips):
                for core in range(2):
                    lo_row = (2 * chip + core) * rows
                    g_ref[chip, core, head, which] = grad[lo_row : lo_row + rows]


def fused_block(query, key_rows, value_rows, rate_rows, mine, other):
    tokens = query.shape[0]
    rates_t = rate_rows.reshape(-1, tokens).T
    chips, heads, mats, rows, dh = mine.shape
    core = (lax.axis_index("tok") % 2).astype(jnp.int32).reshape(1)
    vmem = pl.BlockSpec(memory_space=pltpu.VMEM)
    return pl.pallas_call(
        _block_kernel,
        out_shape=(
            jax.ShapeDtypeStruct(query.shape, jnp.bfloat16),
            jax.ShapeDtypeStruct((chips, 2, heads, mats, rows, dh), jnp.float32),
        ),
        in_specs=[pl.BlockSpec(memory_space=pltpu.SMEM)] + [vmem] * 6,
        out_specs=(vmem, vmem),
        scratch_shapes=[pltpu.VMEM((heads, mats, chips * 2 * rows, dh), jnp.float32)],
        compiler_params=pltpu.CompilerParams(vmem_limit_bytes=48 * 1024 * 1024),
    )(core, query, key_rows, value_rows, rates_t, mine, other)

class Ring:
    def __init__(self, mesh):
        tok = mesh.shape["tok"]
        chips = tok // 2
        coords = [tuple(mesh.devices[0, 2 * c].coords) for c in range(chips)]
        ys = sorted({c[1] for c in coords})
        if len(ys) == 2:
            ahead = sorted((c for c in range(chips) if coords[c][1] == ys[0]), key=lambda c: coords[c][2])
            back = sorted((c for c in range(chips) if coords[c][1] == ys[1]), key=lambda c: -coords[c][2])
            cycle = ahead + back
        else:
            cycle = sorted(range(chips), key=lambda c: (coords[c][1], coords[c][2]))
        self.chips = chips
        self.cycle = cycle
        place = [0] * chips
        for i, c in enumerate(cycle):
            place[c] = i
        self.place = place
        self.cw = [(cycle[p] * 2 + k, cycle[(p + 1) % chips] * 2 + k) for p in range(chips) for k in range(2)]
        self.ccw = [(cycle[p] * 2 + k, cycle[(p - 1) % chips] * 2 + k) for p in range(chips) for k in range(2)]
        self.swap = [(t, t ^ 1) for t in range(tok)]
        self.ncw = chips // 2
        self.nccw = chips - 1 - self.ncw

    def chip_at(self, step):
        me = lax.axis_index("tok") // 2
        where = jnp.array(self.place, jnp.int32)[me]
        return jnp.array(self.cycle, jnp.int32)[(where + step) % self.chips]

    def gather(self, own):
        h, g, rows, f = own.shape
        core = lax.axis_index("tok") % 2
        even = self.chips % 2 == 0
        ring = jnp.zeros((self.chips, h, g, rows, f), own.dtype)
        ring = lax.dynamic_update_index_in_dim(ring, own, lax.axis_index("tok") // 2, 0)
        a = own
        b = own
        last = self.ncw if even else 0
        for k in range(1, max(self.ncw, self.nccw) + 1):
            if k == last:
                a = lax.ppermute(a[..., : f // 2], "tok", self.cw)
                b = lax.ppermute(b[..., f // 2 :], "tok", self.ccw)
                ring = lax.dynamic_update_index_in_dim(ring, jnp.concatenate([a, b], -1), self.chip_at(k), 0)
                continue
            if k <= self.ncw:
                a = lax.ppermute(a, "tok", self.cw)
                ring = lax.dynamic_update_index_in_dim(ring, a, self.chip_at(-k), 0)
            if k <= self.nccw:
                b = lax.ppermute(b, "tok", self.ccw)
                ring = lax.dynamic_update_index_in_dim(ring, b, self.chip_at(k), 0)
        return ring, lax.ppermute(ring, "tok", self.swap)

    def reduce(self, q):
        _, _, h, g, rows, f = q.shape
        core = lax.axis_index("tok") % 2

        def chip_sum(step):
            chip = self.chip_at(step)
            keep = lax.dynamic_slice(q, (chip, core, 0, 0, 0, 0), (1, 1, h, g, rows, f))
            send = lax.dynamic_slice(q, (chip, 1 - core, 0, 0, 0, 0), (1, 1, h, g, rows, f))
            got = lax.ppermute(send, "tok", self.swap)
            return (keep + got).reshape(h, g, rows, f)

        total = chip_sum(0)
        if self.chips % 2 == 0:
            n = self.chips // 2
            half = f // 2
            far = chip_sum(n)
            a = far[..., :half]
            b = far[..., half:]
            for k in range(1, n + 1):
                a = lax.ppermute(a.astype(jnp.bfloat16), "tok", self.cw).astype(jnp.float32)
                b = lax.ppermute(b.astype(jnp.bfloat16), "tok", self.ccw).astype(jnp.float32)
                if k < n:
                    near_a = chip_sum(n - k)
                    near_b = chip_sum(k - n)
                    if k == 1:
                        a = jnp.concatenate([a + near_a[..., :half], near_a[..., half:]], -1)
                        b = jnp.concatenate([near_b[..., :half], b + near_b[..., half:]], -1)
                    else:
                        a = a + near_a
                        b = b + near_b
            if n == 1:
                return total + jnp.concatenate([a, b], -1)
            return total + a + b
        a = chip_sum(self.ncw) if self.ncw else None
        b = chip_sum(-self.nccw) if self.nccw else None
        for k in range(1, max(self.ncw, self.nccw) + 1):
            if k <= self.ncw:
                a = lax.ppermute(a.astype(jnp.bfloat16), "tok", self.cw).astype(jnp.float32)
                if k < self.ncw:
                    a = a + chip_sum(self.ncw - k)
            if k <= self.nccw:
                b = lax.ppermute(b.astype(jnp.bfloat16), "tok", self.ccw).astype(jnp.float32)
                if k < self.nccw:
                    b = b + chip_sum(-self.nccw + k)
        if a is not None:
            total = total + a
        if b is not None:
            total = total + b
        return total


def solution(mesh):
    ring = Ring(mesh)

    def on_device(queries, keys, values, rates, fast_weights):
        nblocks = queries.shape[0]
        own = fast_weights
        blocks = []
        for span in range(nblocks):
            mine, other = ring.gather(own.astype(jnp.bfloat16))
            normed, partial_value = fused_block(queries[span], keys[span], values[span], rates[span], mine, other)
            blocks.append(normed)
            own = renorm(own, own + ring.reduce(partial_value))
        return (jnp.stack(blocks), own)

    placed = (
        P(None, ("groups", "tok"), None),
        P(None, ("groups", "tok"), None),
        P(None, ("groups", "tok"), None),
        P(None, None, None, ("groups", "tok")),
        P(None, None, "tok", None),
    )
    return jax.shard_map(
        on_device,
        mesh=mesh,
        in_specs=placed,
        out_specs=(P(None, ("groups", "tok"), None), P("groups", None, "tok", None)),
        check_vma=False,
    )
```

```python
import jax
import jax.numpy as jnp
from jax import lax
from jax.experimental import pallas as pl
from jax.experimental.pallas import tpu as pltpu
from jax.sharding import PartitionSpec as P


def cross(left, right):
    return lax.dot_general(
        left, right, (((1,), (1,)), ((), ())), preferred_element_type=jnp.float32
    )


def inner(left, right):
    return lax.dot_general(
        left, right, (((0,), (0,)), ((), ())), preferred_element_type=jnp.float32
    )


def renorm(old, upd):
    old_norm = jnp.sqrt(jnp.mean(old * old, axis=-1))
    new_norm = jnp.sqrt(jnp.mean(upd * upd, axis=-1) + 1e-06)
    return upd * (old_norm / new_norm)[..., None]


def head_step(query, key_rows, value_rows, rate_rows, wbf):
    hidden_q = (jax.nn.silu(cross(query, wbf[0])) * cross(query, wbf[1])).astype(jnp.bfloat16)
    raw = cross(hidden_q, wbf[2])
    normed = (raw / jnp.sqrt(jnp.mean(raw * raw, axis=-1, keepdims=True) + 1e-06)).astype(
        jnp.bfloat16
    )
    h1 = cross(key_rows, wbf[0])
    h3 = cross(key_rows, wbf[1])
    sig = jax.nn.sigmoid(h1)
    act = h1 * sig
    back = jnp.dot(value_rows, wbf[2], preferred_element_type=jnp.float32)
    d1 = back * h3 * sig * (1.0 + h1 * (1.0 - sig))
    d3 = back * act
    e1 = (rate_rows[0][:, None] * d1).astype(jnp.bfloat16)
    e3 = (rate_rows[1][:, None] * d3).astype(jnp.bfloat16)
    b2 = (rate_rows[2][:, None] * (act * h3)).astype(jnp.bfloat16)
    grad = jnp.stack([inner(e1, key_rows), inner(e3, key_rows), inner(value_rows, b2)])
    return (normed, grad)


def block_step(span, gathered, queries, keys, values, rates):
    heads = gathered.shape[0]
    width = gathered.shape[3]
    pieces = []
    grads = []
    for head in range(heads):
        lo = head * width
        normed, grad = head_step(
            queries[span][:, lo : lo + width],
            keys[span][:, lo : lo + width],
            values[span][:, lo : lo + width],
            rates[span][:, head],
            gathered[head],
        )
        pieces.append(normed)
        grads.append(grad)
    return (jnp.concatenate(pieces, axis=1), jnp.stack(grads))


def _nt(left, right):
    return lax.dot_general(left, right, (((1,), (1,)), ((), ())), preferred_element_type=jnp.float32)


def _tn(left, right):
    return lax.dot_general(left, right, (((0,), (0,)), ((), ())), preferred_element_type=jnp.float32)


def _block_kernel(core_ref, offs_ref, q_ref, k_ref, v_ref, r_ref, w_ref, o_ref, g_ref):
    heads = w_ref.shape[0]
    width = w_ref.shape[3]
    for head in range(heads):
        lo = head * width
        query = q_ref[:, lo : lo + width]
        key_rows = k_ref[:, lo : lo + width]
        value_rows = v_ref[:, lo : lo + width]
        gate = w_ref[head, 0]
        up = w_ref[head, 1]
        down = w_ref[head, 2]
        a1 = _nt(query, gate)
        a3 = _nt(query, up)
        hidden_q = (a1 / (1.0 + jnp.exp(-a1)) * a3).astype(jnp.bfloat16)
        raw = _nt(hidden_q, down)
        scale = jnp.sqrt(jnp.mean(raw * raw, axis=-1, keepdims=True) + 1e-06)
        o_ref[:, lo : lo + width] = (raw / scale).astype(jnp.bfloat16)
        h1 = _nt(key_rows, gate)
        h3 = _nt(key_rows, up)
        sig = 1.0 / (1.0 + jnp.exp(-h1))
        act = h1 * sig
        back = jnp.dot(value_rows, down, preferred_element_type=jnp.float32)
        d1 = back * h3 * sig * (1.0 + h1 * (1.0 - sig))
        d3 = back * act
        e1 = (r_ref[:, head : head + 1] * d1).astype(jnp.bfloat16)
        e3 = (r_ref[:, heads + head : heads + head + 1] * d3).astype(jnp.bfloat16)
        b2 = (r_ref[:, 2 * heads + head : 2 * heads + head + 1] * (act * h3)).astype(jnp.bfloat16)
        chips = g_ref.shape[1]
        rows = g_ref.shape[4]
        own = core_ref[0]
        for which, grad in enumerate((_tn(e1, key_rows), _tn(e3, key_rows), _tn(value_rows, b2))):
            for chip in range(chips):
                for core in range(2):
                    lo_row = (2 * chip + core) * rows
                    slot = core + own - 2 * core * own
                    g_ref[slot, offs_ref[chip], head, which] = grad[lo_row : lo_row + rows]


def fused_block(query, key_rows, value_rows, rate_rows, wbf, offs):
    tokens = query.shape[0]
    rates_t = rate_rows.reshape(-1, tokens).T
    heads, mats, hid, dh = wbf.shape
    chips = offs.shape[0]
    core = (lax.axis_index("tok") % 2).astype(jnp.int32).reshape(1)
    vmem = pl.BlockSpec(memory_space=pltpu.VMEM)
    smem = pl.BlockSpec(memory_space=pltpu.SMEM)
    return pl.pallas_call(
        _block_kernel,
        out_shape=(
            jax.ShapeDtypeStruct(query.shape, jnp.bfloat16),
            jax.ShapeDtypeStruct((2, chips, heads, mats, hid // (2 * chips), dh), jnp.float32),
        ),
        in_specs=[smem, smem] + [vmem] * 5,
        out_specs=(vmem, vmem),
        compiler_params=pltpu.CompilerParams(vmem_limit_bytes=48 * 1024 * 1024),
    )(core, offs, query, key_rows, value_rows, rates_t, wbf)

class Ring:
    def __init__(self, mesh):
        tok = mesh.shape["tok"]
        chips = tok // 2
        coords = [tuple(mesh.devices[0, 2 * c].coords) for c in range(chips)]
        ys = sorted({c[1] for c in coords})
        if len(ys) == 2:
            ahead = sorted((c for c in range(chips) if coords[c][1] == ys[0]), key=lambda c: coords[c][2])
            back = sorted((c for c in range(chips) if coords[c][1] == ys[1]), key=lambda c: -coords[c][2])
            cycle = ahead + back
        else:
            cycle = sorted(range(chips), key=lambda c: (coords[c][1], coords[c][2]))
        self.chips = chips
        self.cycle = cycle
        place = [0] * chips
        for i, c in enumerate(cycle):
            place[c] = i
        self.place = place
        self.cw = [(cycle[p] * 2 + k, cycle[(p + 1) % chips] * 2 + k) for p in range(chips) for k in range(2)]
        self.ccw = [(cycle[p] * 2 + k, cycle[(p - 1) % chips] * 2 + k) for p in range(chips) for k in range(2)]
        self.swap = [(t, t ^ 1) for t in range(tok)]
        self.ncw = chips // 2
        self.nccw = chips - 1 - self.ncw

    def chip_at(self, step):
        me = lax.axis_index("tok") // 2
        where = jnp.array(self.place, jnp.int32)[me]
        return jnp.array(self.cycle, jnp.int32)[(where + step) % self.chips]

    def gather(self, own):
        h, g, rows, f = own.shape
        core = lax.axis_index("tok") % 2
        even = self.chips % 2 == 0
        ring = jnp.zeros((self.chips, h, g, rows, f), own.dtype)
        ring = lax.dynamic_update_index_in_dim(ring, own, lax.axis_index("tok") // 2, 0)
        a = own
        b = own
        last = self.ncw if even else 0
        for k in range(1, max(self.ncw, self.nccw) + 1):
            if k == last:
                a = lax.ppermute(a[..., : f // 2], "tok", self.cw)
                b = lax.ppermute(b[..., f // 2 :], "tok", self.ccw)
                ring = lax.dynamic_update_index_in_dim(ring, jnp.concatenate([a, b], -1), self.chip_at(k), 0)
                continue
            if k <= self.ncw:
                a = lax.ppermute(a, "tok", self.cw)
                ring = lax.dynamic_update_index_in_dim(ring, a, self.chip_at(-k), 0)
            if k <= self.nccw:
                b = lax.ppermute(b, "tok", self.ccw)
                ring = lax.dynamic_update_index_in_dim(ring, b, self.chip_at(k), 0)
        other = lax.ppermute(ring, "tok", self.swap)
        full = jnp.zeros((self.chips, 2, h, g, rows, f), own.dtype)
        full = lax.dynamic_update_slice(full, ring[:, None], (0, core, 0, 0, 0, 0))
        full = lax.dynamic_update_slice(full, other[:, None], (0, 1 - core, 0, 0, 0, 0))
        full = jnp.moveaxis(full, (0, 1), (2, 3))
        return full.reshape(h, g, self.chips * 2 * rows, f)

    def offsets(self):
        table = [[(self.place[c] - self.place[t // 2]) % self.chips for c in range(self.chips)] for t in range(2 * self.chips)]
        return jnp.array(table, jnp.int32)[lax.axis_index("tok")]

    def reduce(self, q):
        _, _, h, g, rows, f = q.shape

        def chip_sum(step):
            j = step % self.chips
            return q[0, j] + lax.ppermute(q[1, j], "tok", self.swap)

        total = chip_sum(0)
        if self.chips % 2 == 0:
            n = self.chips // 2
            half = f // 2
            far = chip_sum(n)
            a = far[..., :half]
            b = far[..., half:]
            for k in range(1, n + 1):
                a = lax.ppermute(a.astype(jnp.bfloat16), "tok", self.cw).astype(jnp.float32)
                b = lax.ppermute(b.astype(jnp.bfloat16), "tok", self.ccw).astype(jnp.float32)
                if k < n:
                    near_a = chip_sum(n - k)
                    near_b = chip_sum(k - n)
                    if k == 1:
                        a = jnp.concatenate([a + near_a[..., :half], near_a[..., half:]], -1)
                        b = jnp.concatenate([near_b[..., :half], b + near_b[..., half:]], -1)
                    else:
                        a = a + near_a
                        b = b + near_b
            if n == 1:
                return total + jnp.concatenate([a, b], -1)
            return total + a + b
        a = chip_sum(self.ncw) if self.ncw else None
        b = chip_sum(-self.nccw) if self.nccw else None
        for k in range(1, max(self.ncw, self.nccw) + 1):
            if k <= self.ncw:
                a = lax.ppermute(a.astype(jnp.bfloat16), "tok", self.cw).astype(jnp.float32)
                if k < self.ncw:
                    a = a + chip_sum(self.ncw - k)
            if k <= self.nccw:
                b = lax.ppermute(b.astype(jnp.bfloat16), "tok", self.ccw).astype(jnp.float32)
                if k < self.nccw:
                    b = b + chip_sum(-self.nccw + k)
        if a is not None:
            total = total + a
        if b is not None:
            total = total + b
        return total


def solution(mesh):
    ring = Ring(mesh)

    def on_device(queries, keys, values, rates, fast_weights):
        nblocks = queries.shape[0]
        offs = ring.offsets()
        own = fast_weights
        blocks = []
        for span in range(nblocks):
            gathered = ring.gather(own.astype(jnp.bfloat16))
            normed, partial_value = fused_block(queries[span], keys[span], values[span], rates[span], gathered, offs)
            blocks.append(normed)
            own = renorm(own, own + ring.reduce(partial_value))
        return (jnp.stack(blocks), own)

    placed = (
        P(None, ("groups", "tok"), None),
        P(None, ("groups", "tok"), None),
        P(None, ("groups", "tok"), None),
        P(None, None, None, ("groups", "tok")),
        P(None, None, "tok", None),
    )
    return jax.shard_map(
        on_device,
        mesh=mesh,
        in_specs=placed,
        out_specs=(P(None, ("groups", "tok"), None), P("groups", None, "tok", None)),
        check_vma=False,
    )
```

```python
import jax
import jax.numpy as jnp
from jax import lax
from jax.experimental import pallas as pl
from jax.experimental.pallas import tpu as pltpu
from jax.sharding import PartitionSpec as P


def cross(left, right):
    return lax.dot_general(
        left, right, (((1,), (1,)), ((), ())), preferred_element_type=jnp.float32
    )


def inner(left, right):
    return lax.dot_general(
        left, right, (((0,), (0,)), ((), ())), preferred_element_type=jnp.float32
    )


def renorm(old, upd):
    old_norm = jnp.sqrt(jnp.mean(old * old, axis=-1))
    new_norm = jnp.sqrt(jnp.mean(upd * upd, axis=-1) + 1e-06)
    return upd * (old_norm / new_norm)[..., None]


def head_step(query, key_rows, value_rows, rate_rows, wbf):
    hidden_q = (jax.nn.silu(cross(query, wbf[0])) * cross(query, wbf[1])).astype(jnp.bfloat16)
    raw = cross(hidden_q, wbf[2])
    normed = (raw / jnp.sqrt(jnp.mean(raw * raw, axis=-1, keepdims=True) + 1e-06)).astype(
        jnp.bfloat16
    )
    h1 = cross(key_rows, wbf[0])
    h3 = cross(key_rows, wbf[1])
    sig = jax.nn.sigmoid(h1)
    act = h1 * sig
    back = jnp.dot(value_rows, wbf[2], preferred_element_type=jnp.float32)
    d1 = back * h3 * sig * (1.0 + h1 * (1.0 - sig))
    d3 = back * act
    e1 = (rate_rows[0][:, None] * d1).astype(jnp.bfloat16)
    e3 = (rate_rows[1][:, None] * d3).astype(jnp.bfloat16)
    b2 = (rate_rows[2][:, None] * (act * h3)).astype(jnp.bfloat16)
    grad = jnp.stack([inner(e1, key_rows), inner(e3, key_rows), inner(value_rows, b2)])
    return (normed, grad)


def block_step(span, gathered, queries, keys, values, rates):
    heads = gathered.shape[0]
    width = gathered.shape[3]
    pieces = []
    grads = []
    for head in range(heads):
        lo = head * width
        normed, grad = head_step(
            queries[span][:, lo : lo + width],
            keys[span][:, lo : lo + width],
            values[span][:, lo : lo + width],
            rates[span][:, head],
            gathered[head],
        )
        pieces.append(normed)
        grads.append(grad)
    return (jnp.concatenate(pieces, axis=1), jnp.stack(grads))


def _nt(left, right):
    return lax.dot_general(left, right, (((1,), (1,)), ((), ())), preferred_element_type=jnp.float32)


def _tn(left, right):
    return lax.dot_general(left, right, (((0,), (0,)), ((), ())), preferred_element_type=jnp.float32)


def _block_kernel(q_ref, k_ref, v_ref, r_ref, w_ref, o_ref, g_ref):
    heads = w_ref.shape[0]
    width = w_ref.shape[3]
    for head in range(heads):
        lo = head * width
        query = q_ref[:, lo : lo + width]
        key_rows = k_ref[:, lo : lo + width]
        value_rows = v_ref[:, lo : lo + width]
        gate = w_ref[head, 0]
        up = w_ref[head, 1]
        down = w_ref[head, 2]
        a1 = _nt(query, gate)
        a3 = _nt(query, up)
        hidden_q = (a1 / (1.0 + jnp.exp(-a1)) * a3).astype(jnp.bfloat16)
        raw = _nt(hidden_q, down)
        scale = jnp.sqrt(jnp.mean(raw * raw, axis=-1, keepdims=True) + 1e-06)
        o_ref[:, lo : lo + width] = (raw / scale).astype(jnp.bfloat16)
        h1 = _nt(key_rows, gate)
        h3 = _nt(key_rows, up)
        sig = 1.0 / (1.0 + jnp.exp(-h1))
        act = h1 * sig
        back = jnp.dot(value_rows, down, preferred_element_type=jnp.float32)
        d1 = back * h3 * sig * (1.0 + h1 * (1.0 - sig))
        d3 = back * act
        e1 = (r_ref[:, head : head + 1] * d1).astype(jnp.bfloat16)
        e3 = (r_ref[:, heads + head : heads + head + 1] * d3).astype(jnp.bfloat16)
        b2 = (r_ref[:, 2 * heads + head : 2 * heads + head + 1] * (act * h3)).astype(jnp.bfloat16)
        chips = g_ref.shape[0]
        rows = g_ref.shape[4]
        for which, grad in enumerate((_tn(e1, key_rows), _tn(e3, key_rows), _tn(value_rows, b2))):
            for chip in range(chips):
                for core in range(2):
                    lo_row = (2 * chip + core) * rows
                    g_ref[chip, core, head, which] = grad[lo_row : lo_row + rows]


def fused_block(query, key_rows, value_rows, rate_rows, wbf, chips):
    tokens = query.shape[0]
    rates_t = rate_rows.reshape(-1, tokens).T
    heads, mats, hid, dh = wbf.shape
    return pl.pallas_call(
        _block_kernel,
        out_shape=(
            jax.ShapeDtypeStruct(query.shape, jnp.bfloat16),
            jax.ShapeDtypeStruct((chips, 2, heads, mats, hid // (2 * chips), dh), jnp.float32),
        ),
        compiler_params=pltpu.CompilerParams(vmem_limit_bytes=48 * 1024 * 1024),
    )(query, key_rows, value_rows, rates_t, wbf)


class Ring:
    def __init__(self, mesh):
        tok = mesh.shape["tok"]
        chips = tok // 2
        coords = [tuple(mesh.devices[0, 2 * c].coords) for c in range(chips)]
        ys = sorted({c[1] for c in coords})
        if len(ys) == 2:
            ahead = sorted((c for c in range(chips) if coords[c][1] == ys[0]), key=lambda c: coords[c][2])
            back = sorted((c for c in range(chips) if coords[c][1] == ys[1]), key=lambda c: -coords[c][2])
            cycle = ahead + back
        else:
            cycle = sorted(range(chips), key=lambda c: (coords[c][1], coords[c][2]))
        self.chips = chips
        self.cycle = cycle
        place = [0] * chips
        for i, c in enumerate(cycle):
            place[c] = i
        self.place = place
        self.cw = [(cycle[p] * 2 + k, cycle[(p + 1) % chips] * 2 + k) for p in range(chips) for k in range(2)]
        self.ccw = [(cycle[p] * 2 + k, cycle[(p - 1) % chips] * 2 + k) for p in range(chips) for k in range(2)]
        self.swap = [(t, t ^ 1) for t in range(tok)]
        self.ncw = chips // 2
        self.nccw = chips - 1 - self.ncw

    def chip_at(self, step):
        me = lax.axis_index("tok") // 2
        where = jnp.array(self.place, jnp.int32)[me]
        return jnp.array(self.cycle, jnp.int32)[(where + step) % self.chips]

    def gather(self, own):
        h, g, rows, f = own.shape
        core = lax.axis_index("tok") % 2
        even = self.chips % 2 == 0
        ring = jnp.zeros((self.chips, h, g, rows, f), own.dtype)
        ring = lax.dynamic_update_index_in_dim(ring, own, lax.axis_index("tok") // 2, 0)
        a = own
        b = own
        last = self.ncw if even else 0
        for k in range(1, max(self.ncw, self.nccw) + 1):
            if k == last:
                early = lax.ppermute(ring, "tok", self.swap)
                a = lax.ppermute(a[..., : f // 2], "tok", self.cw)
                b = lax.ppermute(b[..., f // 2 :], "tok", self.ccw)
                far = jnp.concatenate([a, b], -1)
                ring = lax.dynamic_update_index_in_dim(ring, far, self.chip_at(k), 0)
                other = lax.dynamic_update_index_in_dim(early, lax.ppermute(far, "tok", self.swap), self.chip_at(k), 0)
                continue
            if k <= self.ncw:
                a = lax.ppermute(a, "tok", self.cw)
                ring = lax.dynamic_update_index_in_dim(ring, a, self.chip_at(-k), 0)
            if k <= self.nccw:
                b = lax.ppermute(b, "tok", self.ccw)
                ring = lax.dynamic_update_index_in_dim(ring, b, self.chip_at(k), 0)
        if not last:
            other = lax.ppermute(ring, "tok", self.swap)
        full = jnp.zeros((self.chips, 2, h, g, rows, f), own.dtype)
        full = lax.dynamic_update_slice(full, ring[:, None], (0, core, 0, 0, 0, 0))
        full = lax.dynamic_update_slice(full, other[:, None], (0, 1 - core, 0, 0, 0, 0))
        full = jnp.moveaxis(full, (0, 1), (2, 3))
        return full.reshape(h, g, self.chips * 2 * rows, f)

    def reduce(self, q):
        _, _, h, g, rows, f = q.shape
        core = lax.axis_index("tok") % 2

        def chip_sum(step):
            chip = self.chip_at(step)
            keep = lax.dynamic_slice(q, (chip, core, 0, 0, 0, 0), (1, 1, h, g, rows, f))
            send = lax.dynamic_slice(q, (chip, 1 - core, 0, 0, 0, 0), (1, 1, h, g, rows, f))
            got = lax.ppermute(send, "tok", self.swap)
            return (keep + got).reshape(h, g, rows, f)

        total = chip_sum(0)
        if self.chips % 2 == 0:
            n = self.chips // 2
            half = f // 2
            far = chip_sum(n)
            a = far[..., :half]
            b = far[..., half:]
            for k in range(1, n + 1):
                a = lax.ppermute(a.astype(jnp.bfloat16), "tok", self.cw).astype(jnp.float32)
                b = lax.ppermute(b.astype(jnp.bfloat16), "tok", self.ccw).astype(jnp.float32)
                if k < n:
                    near_a = chip_sum(n - k)
                    near_b = chip_sum(k - n)
                    if k == 1:
                        a = jnp.concatenate([a + near_a[..., :half], near_a[..., half:]], -1)
                        b = jnp.concatenate([near_b[..., :half], b + near_b[..., half:]], -1)
                    else:
                        a = a + near_a
                        b = b + near_b
            if n == 1:
                return total + jnp.concatenate([a, b], -1)
            return total + a + b
        a = chip_sum(self.ncw) if self.ncw else None
        b = chip_sum(-self.nccw) if self.nccw else None
        for k in range(1, max(self.ncw, self.nccw) + 1):
            if k <= self.ncw:
                a = lax.ppermute(a.astype(jnp.bfloat16), "tok", self.cw).astype(jnp.float32)
                if k < self.ncw:
                    a = a + chip_sum(self.ncw - k)
            if k <= self.nccw:
                b = lax.ppermute(b.astype(jnp.bfloat16), "tok", self.ccw).astype(jnp.float32)
                if k < self.nccw:
                    b = b + chip_sum(-self.nccw + k)
        if a is not None:
            total = total + a
        if b is not None:
            total = total + b
        return total


def solution(mesh):
    ring = Ring(mesh)

    def on_device(queries, keys, values, rates, fast_weights):
        nblocks = queries.shape[0]
        own = fast_weights
        blocks = []
        for span in range(nblocks):
            gathered = ring.gather(own.astype(jnp.bfloat16))
            normed, partial_value = fused_block(queries[span], keys[span], values[span], rates[span], gathered, ring.chips)
            blocks.append(normed)
            own = renorm(own, own + ring.reduce(partial_value))
        return (jnp.stack(blocks), own)

    placed = (
        P(None, ("groups", "tok"), None),
        P(None, ("groups", "tok"), None),
        P(None, ("groups", "tok"), None),
        P(None, None, None, ("groups", "tok")),
        P(None, None, "tok", None),
    )
    return jax.shard_map(
        on_device,
        mesh=mesh,
        in_specs=placed,
        out_specs=(P(None, ("groups", "tok"), None), P("groups", None, "tok", None)),
        check_vma=False,
    )
```

```python
import jax
import jax.numpy as jnp
from jax import lax
from jax.experimental import pallas as pl
from jax.experimental.pallas import tpu as pltpu
from jax.sharding import PartitionSpec as P


def cross(left, right):
    return lax.dot_general(
        left, right, (((1,), (1,)), ((), ())), preferred_element_type=jnp.float32
    )


def inner(left, right):
    return lax.dot_general(
        left, right, (((0,), (0,)), ((), ())), preferred_element_type=jnp.float32
    )


def renorm(old, upd):
    old_norm = jnp.sqrt(jnp.mean(old * old, axis=-1))
    new_norm = jnp.sqrt(jnp.mean(upd * upd, axis=-1) + 1e-06)
    return upd * (old_norm / new_norm)[..., None]


def head_step(query, key_rows, value_rows, rate_rows, wbf):
    hidden_q = (jax.nn.silu(cross(query, wbf[0])) * cross(query, wbf[1])).astype(jnp.bfloat16)
    raw = cross(hidden_q, wbf[2])
    normed = (raw / jnp.sqrt(jnp.mean(raw * raw, axis=-1, keepdims=True) + 1e-06)).astype(
        jnp.bfloat16
    )
    h1 = cross(key_rows, wbf[0])
    h3 = cross(key_rows, wbf[1])
    sig = jax.nn.sigmoid(h1)
    act = h1 * sig
    back = jnp.dot(value_rows, wbf[2], preferred_element_type=jnp.float32)
    d1 = back * h3 * sig * (1.0 + h1 * (1.0 - sig))
    d3 = back * act
    e1 = (rate_rows[0][:, None] * d1).astype(jnp.bfloat16)
    e3 = (rate_rows[1][:, None] * d3).astype(jnp.bfloat16)
    b2 = (rate_rows[2][:, None] * (act * h3)).astype(jnp.bfloat16)
    grad = jnp.stack([inner(e1, key_rows), inner(e3, key_rows), inner(value_rows, b2)])
    return (normed, grad)


def block_step(span, gathered, queries, keys, values, rates):
    heads = gathered.shape[0]
    width = gathered.shape[3]
    pieces = []
    grads = []
    for head in range(heads):
        lo = head * width
        normed, grad = head_step(
            queries[span][:, lo : lo + width],
            keys[span][:, lo : lo + width],
            values[span][:, lo : lo + width],
            rates[span][:, head],
            gathered[head],
        )
        pieces.append(normed)
        grads.append(grad)
    return (jnp.concatenate(pieces, axis=1), jnp.stack(grads))


def _nt(left, right):
    return lax.dot_general(left, right, (((1,), (1,)), ((), ())), preferred_element_type=jnp.float32)


def _tn(left, right):
    return lax.dot_general(left, right, (((0,), (0,)), ((), ())), preferred_element_type=jnp.float32)


def _block_kernel(q_ref, k_ref, v_ref, r_ref, w_ref, o_ref, g_ref):
    heads = w_ref.shape[0]
    width = w_ref.shape[3]
    for head in range(heads):
        lo = head * width
        query = q_ref[:, lo : lo + width]
        key_rows = k_ref[:, lo : lo + width]
        value_rows = v_ref[:, lo : lo + width]
        gate = w_ref[head, 0]
        up = w_ref[head, 1]
        down = w_ref[head, 2]
        a1 = _nt(query, gate)
        a3 = _nt(query, up)
        hidden_q = (a1 / (1.0 + jnp.exp(-a1)) * a3).astype(jnp.bfloat16)
        raw = _nt(hidden_q, down)
        scale = jnp.sqrt(jnp.mean(raw * raw, axis=-1, keepdims=True) + 1e-06)
        o_ref[:, lo : lo + width] = (raw / scale).astype(jnp.bfloat16)
        h1 = _nt(key_rows, gate)
        h3 = _nt(key_rows, up)
        sig = 1.0 / (1.0 + jnp.exp(-h1))
        act = h1 * sig
        back = jnp.dot(value_rows, down, preferred_element_type=jnp.float32)
        d1 = back * h3 * sig * (1.0 + h1 * (1.0 - sig))
        d3 = back * act
        e1 = (r_ref[:, head : head + 1] * d1).astype(jnp.bfloat16)
        e3 = (r_ref[:, heads + head : heads + head + 1] * d3).astype(jnp.bfloat16)
        b2 = (r_ref[:, 2 * heads + head : 2 * heads + head + 1] * (act * h3)).astype(jnp.bfloat16)
        chips = g_ref.shape[0]
        rows = g_ref.shape[4]
        for which, grad in enumerate((_tn(e1, key_rows), _tn(e3, key_rows), _tn(value_rows, b2))):
            for chip in range(chips):
                for core in range(2):
                    lo_row = (2 * chip + core) * rows
                    g_ref[chip, core, head, which] = grad[lo_row : lo_row + rows]


def fused_block(query, key_rows, value_rows, rate_rows, wbf, chips):
    tokens = query.shape[0]
    rates_t = rate_rows.reshape(-1, tokens).T
    heads, mats, hid, dh = wbf.shape
    return pl.pallas_call(
        _block_kernel,
        out_shape=(
            jax.ShapeDtypeStruct(query.shape, jnp.bfloat16),
            jax.ShapeDtypeStruct((chips, 2, heads, mats, hid // (2 * chips), dh), jnp.float32),
        ),
        compiler_params=pltpu.CompilerParams(vmem_limit_bytes=48 * 1024 * 1024),
    )(query, key_rows, value_rows, rates_t, wbf)


class Ring:
    def __init__(self, mesh):
        tok = mesh.shape["tok"]
        chips = tok // 2
        coords = [tuple(mesh.devices[0, 2 * c].coords) for c in range(chips)]
        ys = sorted({c[1] for c in coords})
        if len(ys) == 2:
            ahead = sorted((c for c in range(chips) if coords[c][1] == ys[0]), key=lambda c: coords[c][2])
            back = sorted((c for c in range(chips) if coords[c][1] == ys[1]), key=lambda c: -coords[c][2])
            cycle = ahead + back
        else:
            cycle = sorted(range(chips), key=lambda c: (coords[c][1], coords[c][2]))
        self.chips = chips
        self.cycle = cycle
        place = [0] * chips
        for i, c in enumerate(cycle):
            place[c] = i
        self.place = place
        self.cw = [(cycle[p] * 2 + k, cycle[(p + 1) % chips] * 2 + k) for p in range(chips) for k in range(2)]
        self.ccw = [(cycle[p] * 2 + k, cycle[(p - 1) % chips] * 2 + k) for p in range(chips) for k in range(2)]
        self.swap = [(t, t ^ 1) for t in range(tok)]
        self.ncw = chips // 2
        self.nccw = chips - 1 - self.ncw

    def chip_at(self, step):
        me = lax.axis_index("tok") // 2
        where = jnp.array(self.place, jnp.int32)[me]
        return jnp.array(self.cycle, jnp.int32)[(where + step) % self.chips]

    def gather(self, own, spare=None):
        h, g, rows, f = own.shape
        core = lax.axis_index("tok") % 2
        even = self.chips % 2 == 0
        ring = jnp.zeros((self.chips, h, g, rows, f), own.dtype) if spare is None else spare[0]
        ring = lax.dynamic_update_index_in_dim(ring, own, lax.axis_index("tok") // 2, 0)
        a = own
        b = own
        last = self.ncw if even else 0
        for k in range(1, max(self.ncw, self.nccw) + 1):
            if k == last:
                a = lax.ppermute(a[..., : f // 2], "tok", self.cw)
                b = lax.ppermute(b[..., f // 2 :], "tok", self.ccw)
                ring = lax.dynamic_update_index_in_dim(ring, jnp.concatenate([a, b], -1), self.chip_at(k), 0)
                continue
            if k <= self.ncw:
                a = lax.ppermute(a, "tok", self.cw)
                ring = lax.dynamic_update_index_in_dim(ring, a, self.chip_at(-k), 0)
            if k <= self.nccw:
                b = lax.ppermute(b, "tok", self.ccw)
                ring = lax.dynamic_update_index_in_dim(ring, b, self.chip_at(k), 0)
        other = lax.ppermute(ring, "tok", self.swap)
        full = jnp.zeros((self.chips, 2, h, g, rows, f), own.dtype) if spare is None else spare[1]
        full = lax.dynamic_update_slice(full, ring[:, None], (0, core, 0, 0, 0, 0))
        full = lax.dynamic_update_slice(full, other[:, None], (0, 1 - core, 0, 0, 0, 0))
        gathered = jnp.moveaxis(full, (0, 1), (2, 3)).reshape(h, g, self.chips * 2 * rows, f)
        return gathered, (ring, full)

    def reduce(self, q):
        _, _, h, g, rows, f = q.shape
        core = lax.axis_index("tok") % 2

        def chip_sum(step):
            chip = self.chip_at(step)
            keep = lax.dynamic_slice(q, (chip, core, 0, 0, 0, 0), (1, 1, h, g, rows, f))
            send = lax.dynamic_slice(q, (chip, 1 - core, 0, 0, 0, 0), (1, 1, h, g, rows, f))
            got = lax.ppermute(send, "tok", self.swap)
            return (keep + got).reshape(h, g, rows, f)

        total = chip_sum(0)
        if self.chips % 2 == 0:
            n = self.chips // 2
            half = f // 2
            far = chip_sum(n)
            a = far[..., :half]
            b = far[..., half:]
            for k in range(1, n + 1):
                a = lax.ppermute(a.astype(jnp.bfloat16), "tok", self.cw).astype(jnp.float32)
                b = lax.ppermute(b.astype(jnp.bfloat16), "tok", self.ccw).astype(jnp.float32)
                if k < n:
                    near_a = chip_sum(n - k)
                    near_b = chip_sum(k - n)
                    if k == 1:
                        a = jnp.concatenate([a + near_a[..., :half], near_a[..., half:]], -1)
                        b = jnp.concatenate([near_b[..., :half], b + near_b[..., half:]], -1)
                    else:
                        a = a + near_a
                        b = b + near_b
            if n == 1:
                return total + jnp.concatenate([a, b], -1)
            return total + a + b
        a = chip_sum(self.ncw) if self.ncw else None
        b = chip_sum(-self.nccw) if self.nccw else None
        for k in range(1, max(self.ncw, self.nccw) + 1):
            if k <= self.ncw:
                a = lax.ppermute(a.astype(jnp.bfloat16), "tok", self.cw).astype(jnp.float32)
                if k < self.ncw:
                    a = a + chip_sum(self.ncw - k)
            if k <= self.nccw:
                b = lax.ppermute(b.astype(jnp.bfloat16), "tok", self.ccw).astype(jnp.float32)
                if k < self.nccw:
                    b = b + chip_sum(-self.nccw + k)
        if a is not None:
            total = total + a
        if b is not None:
            total = total + b
        return total


def solution(mesh):
    ring = Ring(mesh)

    def on_device(queries, keys, values, rates, fast_weights):
        nblocks = queries.shape[0]
        spare = None
        own = fast_weights
        blocks = []
        for span in range(nblocks):
            gathered, spare = ring.gather(own.astype(jnp.bfloat16), spare)
            normed, partial_value = fused_block(queries[span], keys[span], values[span], rates[span], gathered, ring.chips)
            blocks.append(normed)
            own = renorm(own, own + ring.reduce(partial_value))
        return (jnp.stack(blocks), own)

    placed = (
        P(None, ("groups", "tok"), None),
        P(None, ("groups", "tok"), None),
        P(None, ("groups", "tok"), None),
        P(None, None, None, ("groups", "tok")),
        P(None, None, "tok", None),
    )
    return jax.shard_map(
        on_device,
        mesh=mesh,
        in_specs=placed,
        out_specs=(P(None, ("groups", "tok"), None), P("groups", None, "tok", None)),
        check_vma=False,
    )
```

```python
import jax
import jax.numpy as jnp
from jax import lax
from jax.experimental import pallas as pl
from jax.experimental.pallas import tpu as pltpu
from jax.sharding import PartitionSpec as P


def cross(left, right):
    return lax.dot_general(
        left, right, (((1,), (1,)), ((), ())), preferred_element_type=jnp.float32
    )


def inner(left, right):
    return lax.dot_general(
        left, right, (((0,), (0,)), ((), ())), preferred_element_type=jnp.float32
    )


def renorm(old, upd):
    old_norm = jnp.sqrt(jnp.mean(old * old, axis=-1))
    new_norm = jnp.sqrt(jnp.mean(upd * upd, axis=-1) + 1e-06)
    return upd * (old_norm / new_norm)[..., None]


def head_step(query, key_rows, value_rows, rate_rows, wbf):
    hidden_q = (jax.nn.silu(cross(query, wbf[0])) * cross(query, wbf[1])).astype(jnp.bfloat16)
    raw = cross(hidden_q, wbf[2])
    normed = (raw / jnp.sqrt(jnp.mean(raw * raw, axis=-1, keepdims=True) + 1e-06)).astype(
        jnp.bfloat16
    )
    h1 = cross(key_rows, wbf[0])
    h3 = cross(key_rows, wbf[1])
    sig = jax.nn.sigmoid(h1)
    act = h1 * sig
    back = jnp.dot(value_rows, wbf[2], preferred_element_type=jnp.float32)
    d1 = back * h3 * sig * (1.0 + h1 * (1.0 - sig))
    d3 = back * act
    e1 = (rate_rows[0][:, None] * d1).astype(jnp.bfloat16)
    e3 = (rate_rows[1][:, None] * d3).astype(jnp.bfloat16)
    b2 = (rate_rows[2][:, None] * (act * h3)).astype(jnp.bfloat16)
    grad = jnp.stack([inner(e1, key_rows), inner(e3, key_rows), inner(value_rows, b2)])
    return (normed, grad)


def block_step(span, gathered, queries, keys, values, rates):
    heads = gathered.shape[0]
    width = gathered.shape[3]
    pieces = []
    grads = []
    for head in range(heads):
        lo = head * width
        normed, grad = head_step(
            queries[span][:, lo : lo + width],
            keys[span][:, lo : lo + width],
            values[span][:, lo : lo + width],
            rates[span][:, head],
            gathered[head],
        )
        pieces.append(normed)
        grads.append(grad)
    return (jnp.concatenate(pieces, axis=1), jnp.stack(grads))


def _nt(left, right):
    return lax.dot_general(left, right, (((1,), (1,)), ((), ())), preferred_element_type=jnp.float32)


def _tn(left, right):
    return lax.dot_general(left, right, (((0,), (0,)), ((), ())), preferred_element_type=jnp.float32)


def _block_kernel(q_ref, k_ref, v_ref, r_ref, w_ref, o_ref, g_ref):
    heads = w_ref.shape[0]
    width = w_ref.shape[3]
    for head in range(heads):
        lo = head * width
        query = q_ref[:, lo : lo + width]
        key_rows = k_ref[:, lo : lo + width]
        value_rows = v_ref[:, lo : lo + width]
        gate = w_ref[head, 0]
        up = w_ref[head, 1]
        down = w_ref[head, 2]
        a1 = _nt(query, gate)
        a3 = _nt(query, up)
        hidden_q = (a1 / (1.0 + jnp.exp(-a1)) * a3).astype(jnp.bfloat16)
        raw = _nt(hidden_q, down)
        scale = jnp.sqrt(jnp.mean(raw * raw, axis=-1, keepdims=True) + 1e-06)
        o_ref[:, lo : lo + width] = (raw / scale).astype(jnp.bfloat16)
        h1 = _nt(key_rows, gate)
        h3 = _nt(key_rows, up)
        sig = 1.0 / (1.0 + jnp.exp(-h1))
        act = h1 * sig
        back = jnp.dot(value_rows, down, preferred_element_type=jnp.float32)
        d1 = back * h3 * sig * (1.0 + h1 * (1.0 - sig))
        d3 = back * act
        e1 = (r_ref[:, head : head + 1] * d1).astype(jnp.bfloat16)
        e3 = (r_ref[:, heads + head : heads + head + 1] * d3).astype(jnp.bfloat16)
        b2 = (r_ref[:, 2 * heads + head : 2 * heads + head + 1] * (act * h3)).astype(jnp.bfloat16)
        chips = g_ref.shape[0]
        rows = g_ref.shape[4]
        for which, grad in enumerate((_tn(e1, key_rows), _tn(e3, key_rows), _tn(value_rows, b2))):
            for chip in range(chips):
                for core in range(2):
                    lo_row = (2 * chip + core) * rows
                    g_ref[chip, core, head, which] = grad[lo_row : lo_row + rows]


def fused_block(query, key_rows, value_rows, rate_rows, wbf, chips):
    tokens = query.shape[0]
    rates_t = rate_rows.reshape(-1, tokens).T
    heads, mats, hid, dh = wbf.shape
    return pl.pallas_call(
        _block_kernel,
        out_shape=(
            jax.ShapeDtypeStruct(query.shape, jnp.bfloat16),
            jax.ShapeDtypeStruct((chips, 2, heads, mats, hid // (2 * chips), dh), jnp.float32),
        ),
        compiler_params=pltpu.CompilerParams(vmem_limit_bytes=48 * 1024 * 1024),
    )(query, key_rows, value_rows, rates_t, wbf)


class Ring:
    def __init__(self, mesh):
        tok = mesh.shape["tok"]
        chips = tok // 2
        coords = [tuple(mesh.devices[0, 2 * c].coords) for c in range(chips)]
        ys = sorted({c[1] for c in coords})
        if len(ys) == 2:
            ahead = sorted((c for c in range(chips) if coords[c][1] == ys[0]), key=lambda c: coords[c][2])
            back = sorted((c for c in range(chips) if coords[c][1] == ys[1]), key=lambda c: -coords[c][2])
            cycle = ahead + back
        else:
            cycle = sorted(range(chips), key=lambda c: (coords[c][1], coords[c][2]))
        self.chips = chips
        self.cycle = cycle
        place = [0] * chips
        for i, c in enumerate(cycle):
            place[c] = i
        self.place = place
        self.cw = [(cycle[p] * 2 + k, cycle[(p + 1) % chips] * 2 + k) for p in range(chips) for k in range(2)]
        self.ccw = [(cycle[p] * 2 + k, cycle[(p - 1) % chips] * 2 + k) for p in range(chips) for k in range(2)]
        self.swap = [(t, t ^ 1) for t in range(tok)]
        self.ncw = chips // 2
        self.nccw = chips - 1 - self.ncw

    def chip_at(self, step):
        me = lax.axis_index("tok") // 2
        where = jnp.array(self.place, jnp.int32)[me]
        return jnp.array(self.cycle, jnp.int32)[(where + step) % self.chips]

    def gather(self, own):
        h, g, rows, f = own.shape
        core = lax.axis_index("tok") % 2
        even = self.chips % 2 == 0
        ring = jnp.zeros((self.chips, h, g, rows, f), own.dtype)
        ring = lax.dynamic_update_index_in_dim(ring, own, lax.axis_index("tok") // 2, 0)
        a = own
        b = own
        last = self.ncw if even else 0
        for k in range(1, max(self.ncw, self.nccw) + 1):
            if k == last:
                a = lax.ppermute(a[..., : f // 2], "tok", self.cw)
                b = lax.ppermute(b[..., f // 2 :], "tok", self.ccw)
                ring = lax.dynamic_update_index_in_dim(ring, jnp.concatenate([a, b], -1), self.chip_at(k), 0)
                continue
            if k <= self.ncw:
                a = lax.ppermute(a, "tok", self.cw)
                ring = lax.dynamic_update_index_in_dim(ring, a, self.chip_at(-k), 0)
            if k <= self.nccw:
                b = lax.ppermute(b, "tok", self.ccw)
                ring = lax.dynamic_update_index_in_dim(ring, b, self.chip_at(k), 0)
        other = lax.ppermute(ring, "tok", self.swap)
        full = jnp.zeros((self.chips, 2, h, g, rows, f), own.dtype)
        full = lax.dynamic_update_slice(full, ring[:, None], (0, core, 0, 0, 0, 0))
        full = lax.dynamic_update_slice(full, other[:, None], (0, 1 - core, 0, 0, 0, 0))
        full = jnp.moveaxis(full, (0, 1), (2, 3))
        return full.reshape(h, g, self.chips * 2 * rows, f)

    def reduce(self, q):
        _, _, h, g, rows, f = q.shape
        core = lax.axis_index("tok") % 2

        def chip_sum(step):
            chip = self.chip_at(step)
            keep = lax.dynamic_slice(q, (chip, core, 0, 0, 0, 0), (1, 1, h, g, rows, f))
            send = lax.dynamic_slice(q, (chip, 1 - core, 0, 0, 0, 0), (1, 1, h, g, rows, f))
            got = lax.ppermute(send.astype(jnp.bfloat16), "tok", self.swap).astype(jnp.float32)
            return (keep + got).reshape(h, g, rows, f)

        total = chip_sum(0)
        if self.chips % 2 == 0:
            n = self.chips // 2
            half = f // 2
            far = chip_sum(n)
            a = far[..., :half]
            b = far[..., half:]
            for k in range(1, n + 1):
                a = lax.ppermute(a.astype(jnp.bfloat16), "tok", self.cw).astype(jnp.float32)
                b = lax.ppermute(b.astype(jnp.bfloat16), "tok", self.ccw).astype(jnp.float32)
                if k < n:
                    near_a = chip_sum(n - k)
                    near_b = chip_sum(k - n)
                    if k == 1:
                        a = jnp.concatenate([a + near_a[..., :half], near_a[..., half:]], -1)
                        b = jnp.concatenate([near_b[..., :half], b + near_b[..., half:]], -1)
                    else:
                        a = a + near_a
                        b = b + near_b
            if n == 1:
                return total + jnp.concatenate([a, b], -1)
            return total + a + b
        a = chip_sum(self.ncw) if self.ncw else None
        b = chip_sum(-self.nccw) if self.nccw else None
        for k in range(1, max(self.ncw, self.nccw) + 1):
            if k <= self.ncw:
                a = lax.ppermute(a.astype(jnp.bfloat16), "tok", self.cw).astype(jnp.float32)
                if k < self.ncw:
                    a = a + chip_sum(self.ncw - k)
            if k <= self.nccw:
                b = lax.ppermute(b.astype(jnp.bfloat16), "tok", self.ccw).astype(jnp.float32)
                if k < self.nccw:
                    b = b + chip_sum(-self.nccw + k)
        if a is not None:
            total = total + a
        if b is not None:
            total = total + b
        return total


def solution(mesh):
    ring = Ring(mesh)

    def on_device(queries, keys, values, rates, fast_weights):
        nblocks = queries.shape[0]
        own = fast_weights
        blocks = []
        for span in range(nblocks):
            gathered = ring.gather(own.astype(jnp.bfloat16))
            normed, partial_value = fused_block(queries[span], keys[span], values[span], rates[span], gathered, ring.chips)
            blocks.append(normed)
            own = renorm(own, own + ring.reduce(partial_value))
        return (jnp.stack(blocks), own)

    placed = (
        P(None, ("groups", "tok"), None),
        P(None, ("groups", "tok"), None),
        P(None, ("groups", "tok"), None),
        P(None, None, None, ("groups", "tok")),
        P(None, None, "tok", None),
    )
    return jax.shard_map(
        on_device,
        mesh=mesh,
        in_specs=placed,
        out_specs=(P(None, ("groups", "tok"), None), P("groups", None, "tok", None)),
        check_vma=False,
    )
```
